32 devices in a mesh: node: 8 (over z, x), feat: 4 (over y, core).
Axes of the slice: x: 2, y: 2, z: 4, core: 2. Of those that a mesh axis runs over, the one named last changes fastest.
Arguments:
- features: bfloat16 [128, 128, 128], P('node', 'feat'), may hold values from -6 to 6
- tile_values: bfloat16 [2048, 128, 128], P('node'), may hold values from -0.125 to 0.125
- tile_row: int32 [2048], P('node'), may hold values from 0 to 127, as said below
- tile_col: int32 [2048], P('node'), may hold values from 0 to 127, as said below
- tile_count: int32 [8], P('node'), may hold values from 32 to 256, as said below
- weight: float32 [128, 128], P('feat'), may hold values from -0.5 to 0.5
- first_moment: float32 [128, 128], P('feat'), may hold values from -3 to 3
- second_moment: float32 [128, 128], P('feat'), may hold values from 0.1 to 2
- cotangent: bfloat16 [128, 128, 128], P('node', 'feat'), may hold values from -6 to 6
Outputs:
- activated: bfloat16 [128, 128, 128], P('node', 'feat')
- feature_grad: float32 [128, 128, 128], P('node', 'feat')
- new_weight: float32 [128, 128], P('feat')
- new_first: float32 [128, 128], P('feat')
- new_second: float32 [128, 128], P('feat')
The draws below stay inside these ranges and needn't reach their ends.
Inputs may be any that keep to these rules, and one draw needn't show every extreme that they name: `tile_row`: the slots of index d of node (slots d * 256 to (d + 1) * 256 - 1) name target blocks of that index only: d * 16 to (d + 1) * 16 - 1. `tile_col`: A slot's source block lies on an index of node at most 2 away from the slot's own index around the closed loop of node indices; both distances 2 occur on every index. `tile_count`: some index of node has all 256 slots live, some has 32.
All inputs are finite; a program needn't handle non-finite values.
Results may differ from the reference program's by a relative error of at most 0.0058.
Values may be sent and summed in bfloat16 or wider, within the bound.
No kernel may reach another device: no remote copies, remote signals or barrier semaphores. Data moves between devices by JAX's collectives and lax.ppermute only.
A program may use at most 64 MiB of HBM per device.

```python
import math
import jax
import jax.numpy as jnp
from jax import lax

F = 128
TILE = 128
BPD = 16
TILES_BLK = 16
REACH = 2
TCAP = 256
NBLK = 128
TILES = 2048
NODES = 16384
N_NODE = 8


def draw_tile_count(key, part):
    base = jax.random.randint(jax.random.fold_in(key, 11), (N_NODE,), TCAP // 8, TCAP // 2 + 1)
    heavy = jax.random.randint(jax.random.fold_in(key, 12), (N_NODE,), 0, 8) == 0
    chosen = jax.random.randint(jax.random.fold_in(key, 13), (), 0, N_NODE)
    lightest = (chosen + 1 + jax.random.randint(jax.random.fold_in(key, 14), (), 0, N_NODE - 1)) % N_NODE
    position = jnp.arange(N_NODE)
    counts = jnp.where(heavy | (position == chosen), TCAP, base)
    counts = jnp.where(position == lightest, TCAP // 8, counts)
    return counts.astype(jnp.int32)


def draw_tile_row(key, part):
    total = TCAP * N_NODE
    owner = jnp.arange(total) // TCAP
    within = jnp.arange(total) % TCAP
    block = jax.random.randint(jax.random.fold_in(key, 21), (total,), 0, BPD)
    block = jnp.where(within == 2, BPD - 1, jnp.where(within == 3, 0, block))
    return (owner * BPD + block).astype(jnp.int32)


def draw_tile_col(key, part):
    total = TCAP * N_NODE
    owner = jnp.arange(total) // TCAP
    within = jnp.arange(total) % TCAP
    offset = jax.random.randint(jax.random.fold_in(key, 31), (total,), -REACH, REACH + 1)
    offset = jnp.where(within == 0, -REACH, jnp.where(within == 1, REACH, offset))
    block = jax.random.randint(jax.random.fold_in(key, 32), (total,), 0, BPD)
    block = jnp.where(within == 0, 0, jnp.where(within == 1, BPD - 1, block))
    return ((owner + offset) % N_NODE * BPD + block).astype(jnp.int32)


def steps_of(own_key, extent, shards, smallest, top_value):
    gain, own = 1.0, jax.random.fold_in(own_key, 6)
    for dim, parts in shards:
        draws = jnp.exp(jax.random.uniform(jax.random.fold_in(own, dim), (parts,), jnp.float32, smallest / len(shards), top_value / len(shards)))
        gain = gain * jnp.repeat(draws, extent[dim] // parts).reshape([-1 if axis == dim else 1 for axis in range(len(extent))])
    return gain


def gaussian(rng, shape, deviation, reach, pieces=(), held_as=jnp.bfloat16):
    gain = steps_of(rng, shape, pieces, -0.22, 0.18) if pieces else 1.0
    values = jax.random.normal(rng, shape, jnp.float32) * deviation * gain
    return jnp.minimum(jnp.maximum(values, -reach), reach).astype(held_as)


def setup_inputs(seed: int = 0) -> dict:
    splits = jax.random.split(jax.random.key(seed), 10)
    features = gaussian(splits[0], (NBLK, F, TILE), 1.0, 6.0, ((0, 8), (1, 4)))
    tile_values = gaussian(splits[1], (TILES, TILE, TILE), (TILES_BLK * TILE) ** -0.5, 0.125, ((0, 8),))
    tile_row = draw_tile_row(jax.random.fold_in(splits[9], 71), 0)
    tile_col = draw_tile_col(jax.random.fold_in(splits[9], 71), 0)
    tile_count = draw_tile_count(jax.random.fold_in(splits[9], 71), 0)
    weight = gaussian(splits[5], (F, F), F ** -0.5, 0.5, ((0, 4),), jnp.float32)
    first_moment = gaussian(splits[6], (F, F), 0.5, 3.0, ((0, 4),), jnp.float32)
    second_moment = jnp.clip(jnp.exp(math.log(2.0) - 2.9957323 * jax.random.uniform(splits[7], (F, F), jnp.float32) ** steps_of(splits[7], (F, F), ((0, 4),), -0.2, 0.2)), 0.1, 2.0)
    cotangent = gaussian(splits[8], (NBLK, F, TILE), 1.0, 6.0, ((0, 8), (1, 4)))
    return {"features": features, "tile_values": tile_values, "tile_row": tile_row, "tile_col": tile_col, "tile_count": tile_count, "weight": weight, "first_moment": first_moment, "second_moment": second_moment, "cotangent": cotangent}


first_decay = 0.9
second_decay = 0.999
learn_rate = 0.05
first_fix = 1.0 - 0.9 ** 10
second_fix = 1.0 - 0.999 ** 10
adam_eps = 1e-08

def elu_slope(preact):
    return jnp.where(preact > 0, 1.0, jnp.exp(jnp.minimum(preact, 0.0)))

def reference(features, tile_values, tile_row, tile_col, tile_count, weight, first_moment, second_moment, cotangent):
    positions = jnp.arange(TILES)
    owners = positions // TCAP
    live = (positions % TCAP < tile_count[owners]).astype(jnp.float32)
    stacked = (tile_values.reshape(N_NODE, TCAP, TILE, TILE), tile_row.reshape(N_NODE, TCAP), tile_col.reshape(N_NODE, TCAP), live.reshape(N_NODE, TCAP))

    def forward_step(total, items):
        tiles_now, rows_now, cols_now, live_now = items
        sources = features[cols_now].astype(jnp.float32)
        terms = jnp.einsum('tfk,tjk->tfj', sources, tiles_now.astype(jnp.float32), precision=lax.Precision.HIGHEST)
        terms = terms * live_now[:, None, None]
        return (total.at[rows_now].add(terms), None)
    zero_blocks = jnp.zeros((NBLK, F, TILE), jnp.float32)
    aggregate = lax.scan(forward_step, zero_blocks, stacked)[0].astype(jnp.bfloat16)
    weight_half = weight.astype(jnp.bfloat16)
    preact = jnp.einsum('bij,io->boj', aggregate.astype(jnp.float32), weight_half.astype(jnp.float32), precision=lax.Precision.HIGHEST)
    activated = jax.nn.elu(preact).astype(jnp.bfloat16)
    slope_grad = (cotangent.astype(jnp.float32) * elu_slope(preact)).astype(jnp.bfloat16)
    grad = jnp.einsum('bij,boj->io', aggregate.astype(jnp.float32), slope_grad.astype(jnp.float32), precision=lax.Precision.HIGHEST)
    grad = grad * (1.0 / math.sqrt(NODES))
    back_rows = jnp.einsum('io,boj->bij', weight_half.astype(jnp.float32), slope_grad.astype(jnp.float32), precision=lax.Precision.HIGHEST).astype(jnp.bfloat16)

    def backward_step(total, items):
        tiles_now, rows_now, cols_now, live_now = items
        sources = back_rows[rows_now].astype(jnp.float32)
        terms = jnp.einsum('tfj,tjk->tfk', sources, tiles_now.astype(jnp.float32), precision=lax.Precision.HIGHEST)
        terms = terms * live_now[:, None, None]
        return (total.at[cols_now].add(terms), None)
    feature_grad = lax.scan(backward_step, zero_blocks, stacked)[0]
    new_first = first_decay * first_moment + (1.0 - first_decay) * grad
    new_second = second_decay * second_moment + (1.0 - second_decay) * grad * grad
    new_weight = weight - learn_rate * (new_first / first_fix) / (jnp.sqrt(new_second / second_fix) + adam_eps)
    return (activated, feature_grad, new_weight, new_first, new_second)
```

```python
import math

import jax
import jax.numpy as jnp
from jax import lax
from jax.sharding import PartitionSpec as P

REACH = 2


first_decay = 0.9
second_decay = 0.999
learn_rate = 0.05
first_fix = 1.0 - 0.9**10
second_fix = 1.0 - 0.999**10
adam_eps = 1e-08


def passed_along(block, axis, distance):
    devices = range(lax.axis_size(axis))
    route = [((i - distance) % len(devices), i) for i in devices]
    return lax.ppermute(block, axis, route)


def gathered_along(block, axis, dim):
    size = lax.axis_size(axis)
    own = lax.axis_index(axis)
    width = block.shape[dim]
    shape = list(block.shape)
    shape[dim] = size * width
    whole = jnp.zeros(shape, block.dtype)
    for step in range(size):
        piece = block if step == 0 else passed_along(block, axis, -step)
        whole = lax.dynamic_update_slice_in_dim(whole, piece, ((own + step) % size) * width, dim)
    return whole


def summed_over(block, axis):
    size = lax.axis_size(axis)
    if size & (size - 1):
        return lax.psum(block, axis)
    mask = 1
    while mask < size:
        block = block + lax.ppermute(block, axis, [(i, i ^ mask) for i in range(size)])
        mask *= 2
    return block


def elu_slope(preact):
    return jnp.where(preact > 0, 1.0, jnp.exp(jnp.minimum(preact, 0.0)))


def one_hot_table(indices, count, dtype):
    return (indices[:, None] == jnp.arange(count)[None, :]).astype(dtype)


def per_device(
    features,
    tile_values,
    tile_row,
    tile_col,
    tile_count,
    weight,
    first_moment,
    second_moment,
    cotangent,
):
    cycle_size = lax.axis_size("node")
    own_node = lax.axis_index("node")
    blocks = features.shape[0]
    width_local = features.shape[1]
    tile_size = features.shape[2]
    slots = tile_values.shape[0]
    live = (jnp.arange(slots) < tile_count[0]).astype(jnp.float32)
    local_row = tile_row - own_node * blocks
    col_owner = tile_col // blocks
    col_block = tile_col % blocks
    offset = (col_owner - own_node) % cycle_size
    offset = jnp.where(offset > cycle_size // 2, offset - cycle_size, offset)
    source_slot = (offset + REACH) * blocks + col_block
    targets = (2 * REACH + 1) * blocks
    pick_source = one_hot_table(source_slot, targets, jnp.bfloat16)
    pick_row = one_hot_table(local_row, blocks, jnp.bfloat16)
    add_row = one_hot_table(local_row, blocks, jnp.float32) * live[:, None]
    add_source = one_hot_table(source_slot, targets, jnp.float32) * live[:, None]
    pieces = []
    for distance in range(-REACH, REACH + 1):
        if distance == 0:
            pieces.append(features)
        else:
            pieces.append(passed_along(features, "node", -distance))
    nearby = jnp.concatenate(pieces, axis=0)
    sources = jnp.einsum(
        "ts,sfk->tfk", pick_source, nearby, preferred_element_type=jnp.float32
    ).astype(jnp.bfloat16)
    forward_terms = jnp.einsum(
        "tfk,tjk->tfj", sources, tile_values, preferred_element_type=jnp.float32
    )
    aggregate = jnp.einsum("tb,tfj->bfj", add_row, forward_terms, precision=lax.Precision.HIGHEST)
    aggregate = aggregate.astype(jnp.bfloat16)
    weight_half = weight.astype(jnp.bfloat16)
    aggregate_all = gathered_along(aggregate, "feat", 1)
    weight_all = gathered_along(weight_half, "feat", 0)
    cotangent_all = gathered_along(cotangent, "feat", 1)
    column_start = lax.axis_index("feat") * width_local
    preact = jnp.einsum(
        "bij,io->boj", aggregate_all, weight_all, preferred_element_type=jnp.float32
    )
    activated = lax.dynamic_slice_in_dim(jax.nn.elu(preact), column_start, width_local, 1)
    activated = activated.astype(jnp.bfloat16)
    slope_all = (cotangent_all.astype(jnp.float32) * elu_slope(preact)).astype(jnp.bfloat16)
    node_total = cycle_size * blocks * tile_size
    grad_local = jnp.einsum("bij,boj->io", aggregate, slope_all, preferred_element_type=jnp.float32)
    grad = summed_over(grad_local, "node") * (1.0 / math.sqrt(node_total))
    back_rows = jnp.einsum(
        "io,boj->bij", weight_half, slope_all, preferred_element_type=jnp.float32
    ).astype(jnp.bfloat16)
    back_sources = jnp.einsum(
        "tb,bfj->tfj", pick_row, back_rows, preferred_element_type=jnp.float32
    ).astype(jnp.bfloat16)
    back_terms = jnp.einsum(
        "tfj,tjk->tfk", back_sources, tile_values, preferred_element_type=jnp.float32
    )
    outgoing = jnp.einsum("ts,tfk->sfk", add_source, back_terms, precision=lax.Precision.HIGHEST)
    outgoing = outgoing.reshape(2 * REACH + 1, blocks, width_local, tile_size)
    feature_grad = outgoing[REACH]
    for distance in range(-REACH, REACH + 1):
        if distance != 0:
            feature_grad = feature_grad + passed_along(outgoing[distance + REACH], "node", distance)
    new_first = first_decay * first_moment + (1.0 - first_decay) * grad
    new_second = second_decay * second_moment + (1.0 - second_decay) * grad * grad
    new_weight = weight - learn_rate * (new_first / first_fix) / (
        jnp.sqrt(new_second / second_fix) + adam_eps
    )
    return (activated, feature_grad, new_weight, new_first, new_second)


def solution(mesh):
    return jax.shard_map(
        per_device,
        mesh=mesh,
        in_specs=(
            P("node", "feat", None),
            P("node", None, None),
            P("node"),
            P("node"),
            P("node"),
            P("feat", None),
            P("feat", None),
            P("feat", None),
            P("node", "feat", None),
        ),
        out_specs=(
            P("node", "feat", None),
            P("node", "feat", None),
            P("feat", None),
            P("feat", None),
            P("feat", None),
        ),
        check_vma=False,
    )
```

```python
import math

import jax
import jax.numpy as jnp
from jax import lax
from jax.sharding import PartitionSpec as P

REACH = 2


first_decay = 0.9
second_decay = 0.999
learn_rate = 0.05
first_fix = 1.0 - 0.9**10
second_fix = 1.0 - 0.999**10
adam_eps = 1e-08


def passed_along(block, axis, distance):
    devices = range(lax.axis_size(axis))
    route = [((i - distance) % len(devices), i) for i in devices]
    return lax.ppermute(block, axis, route)


def gathered_along(block, axis, dim):
    size = lax.axis_size(axis)
    own = lax.axis_index(axis)
    width = block.shape[dim]
    shape = list(block.shape)
    shape[dim] = size * width
    whole = jnp.zeros(shape, block.dtype)
    for step in range(size):
        piece = block if step == 0 else passed_along(block, axis, -step)
        whole = lax.dynamic_update_slice_in_dim(whole, piece, ((own + step) % size) * width, dim)
    return whole


def summed_over(block, axis):
    size = lax.axis_size(axis)
    if size & (size - 1):
        return lax.psum(block, axis)
    mask = 1
    while mask < size:
        block = block + lax.ppermute(block, axis, [(i, i ^ mask) for i in range(size)])
        mask *= 2
    return block


def elu_slope(preact):
    return jnp.where(preact > 0, 1.0, jnp.exp(jnp.minimum(preact, 0.0)))


def one_hot_table(indices, count, dtype):
    return (indices[:, None] == jnp.arange(count)[None, :]).astype(dtype)


def per_device(
    features,
    tile_values,
    tile_row,
    tile_col,
    tile_count,
    weight,
    first_moment,
    second_moment,
    cotangent,
):
    cycle_size = lax.axis_size("node")
    own_node = lax.axis_index("node")
    blocks = features.shape[0]
    width_local = features.shape[1]
    tile_size = features.shape[2]
    slots = tile_values.shape[0]
    live = (jnp.arange(slots) < tile_count[0]).astype(jnp.float32)
    local_row = tile_row - own_node * blocks
    col_owner = tile_col // blocks
    col_block = tile_col % blocks
    offset = (col_owner - own_node) % cycle_size
    offset = jnp.where(offset > cycle_size // 2, offset - cycle_size, offset)
    source_slot = (offset + REACH) * blocks + col_block
    targets = (2 * REACH + 1) * blocks
    pick_source = one_hot_table(source_slot, targets, jnp.bfloat16)
    pick_row = one_hot_table(local_row, blocks, jnp.bfloat16)
    add_row = one_hot_table(local_row, blocks, jnp.float32) * live[:, None]
    add_source = one_hot_table(source_slot, targets, jnp.float32) * live[:, None]
    pieces = []
    for distance in range(-REACH, REACH + 1):
        if distance == 0:
            pieces.append(features)
        else:
            pieces.append(passed_along(features, "node", -distance))
    nearby = jnp.concatenate(pieces, axis=0)
    sources = jnp.einsum(
        "ts,sfk->tfk", pick_source, nearby, preferred_element_type=jnp.float32
    ).astype(jnp.bfloat16)
    forward_terms = jnp.einsum(
        "tfk,tjk->tfj", sources, tile_values, preferred_element_type=jnp.float32
    )
    aggregate = jnp.einsum("tb,tfj->bfj", add_row, forward_terms, precision=lax.Precision.HIGHEST)
    aggregate = aggregate.astype(jnp.bfloat16)
    weight_half = weight.astype(jnp.bfloat16)
    packed = jnp.concatenate([aggregate, cotangent, weight_half[None]], axis=0)
    packed_all = gathered_along(packed, "feat", 1)
    aggregate_all = packed_all[:blocks]
    cotangent_all = packed_all[blocks : 2 * blocks]
    weight_all = packed_all[2 * blocks]
    column_start = lax.axis_index("feat") * width_local
    preact = jnp.einsum(
        "bij,io->boj", aggregate_all, weight_all, preferred_element_type=jnp.float32
    )
    activated = lax.dynamic_slice_in_dim(jax.nn.elu(preact), column_start, width_local, 1)
    activated = activated.astype(jnp.bfloat16)
    slope_all = (cotangent_all.astype(jnp.float32) * elu_slope(preact)).astype(jnp.bfloat16)
    node_total = cycle_size * blocks * tile_size
    grad_local = jnp.einsum("bij,boj->io", aggregate, slope_all, preferred_element_type=jnp.float32)
    grad = summed_over(grad_local, "node") * (1.0 / math.sqrt(node_total))
    back_rows = jnp.einsum(
        "io,boj->bij", weight_half, slope_all, preferred_element_type=jnp.float32
    ).astype(jnp.bfloat16)
    back_sources = jnp.einsum(
        "tb,bfj->tfj", pick_row, back_rows, preferred_element_type=jnp.float32
    ).astype(jnp.bfloat16)
    back_terms = jnp.einsum(
        "tfj,tjk->tfk", back_sources, tile_values, preferred_element_type=jnp.float32
    )
    outgoing = jnp.einsum("ts,tfk->sfk", add_source, back_terms, precision=lax.Precision.HIGHEST)
    outgoing = outgoing.reshape(2 * REACH + 1, blocks, width_local, tile_size)
    outgoing, grad = lax.optimization_barrier((outgoing, grad))
    feature_grad = outgoing[REACH]
    for distance in range(-REACH, REACH + 1):
        if distance != 0:
            feature_grad = feature_grad + passed_along(outgoing[distance + REACH], "node", distance)
    new_first = first_decay * first_moment + (1.0 - first_decay) * grad
    new_second = second_decay * second_moment + (1.0 - second_decay) * grad * grad
    new_weight = weight - learn_rate * (new_first / first_fix) / (
        jnp.sqrt(new_second / second_fix) + adam_eps
    )
    return (activated, feature_grad, new_weight, new_first, new_second)


def solution(mesh):
    return jax.shard_map(
        per_device,
        mesh=mesh,
        in_specs=(
            P("node", "feat", None),
            P("node", None, None),
            P("node"),
            P("node"),
            P("node"),
            P("feat", None),
            P("feat", None),
            P("feat", None),
            P("node", "feat", None),
        ),
        out_specs=(
            P("node", "feat", None),
            P("node", "feat", None),
            P("feat", None),
            P("feat", None),
            P("feat", None),
        ),
        check_vma=False,
    )
```

```python
import math

import jax
import jax.numpy as jnp
from jax import lax
from jax.sharding import PartitionSpec as P

REACH = 2


first_decay = 0.9
second_decay = 0.999
learn_rate = 0.05
first_fix = 1.0 - 0.9**10
second_fix = 1.0 - 0.999**10
adam_eps = 1e-08


def passed_along(block, axis, distance):
    devices = range(lax.axis_size(axis))
    route = [((i - distance) % len(devices), i) for i in devices]
    return lax.ppermute(block, axis, route)


def gathered_along(block, axis, dim):
    size = lax.axis_size(axis)
    own = lax.axis_index(axis)
    width = block.shape[dim]
    if size & (size - 1):
        pieces = [(block, own)]
        for step in range(1, size):
            pieces.append((passed_along(block, axis, -step), (own + step) % size))
    else:
        pieces = [(block, own)]
        mask = size // 2
        while mask >= 1:
            held = jnp.stack([piece for piece, _ in pieces])
            got = lax.ppermute(held, axis, [(i, i ^ mask) for i in range(size)])
            pieces = pieces + [(got[k], index ^ mask) for k, (_, index) in enumerate(pieces)]
            mask //= 2
    shape = list(block.shape)
    shape[dim] = size * width
    whole = jnp.zeros(shape, block.dtype)
    for piece, index in pieces:
        whole = lax.dynamic_update_slice_in_dim(whole, piece, index * width, dim)
    return whole


def summed_over(block, axis):
    size = lax.axis_size(axis)
    if size & (size - 1):
        return lax.psum(block, axis)
    mask = 1
    while mask < size:
        block = block + lax.ppermute(block, axis, [(i, i ^ mask) for i in range(size)])
        mask *= 2
    return block


def elu_slope(preact):
    return jnp.where(preact > 0, 1.0, jnp.exp(jnp.minimum(preact, 0.0)))


def one_hot_table(indices, count, dtype):
    return (indices[:, None] == jnp.arange(count)[None, :]).astype(dtype)


def per_device(
    features,
    tile_values,
    tile_row,
    tile_col,
    tile_count,
    weight,
    first_moment,
    second_moment,
    cotangent,
):
    cycle_size = lax.axis_size("node")
    own_node = lax.axis_index("node")
    blocks = features.shape[0]
    width_local = features.shape[1]
    tile_size = features.shape[2]
    slots = tile_values.shape[0]
    live = (jnp.arange(slots) < tile_count[0]).astype(jnp.float32)
    local_row = tile_row - own_node * blocks
    col_owner = tile_col // blocks
    col_block = tile_col % blocks
    offset = (col_owner - own_node) % cycle_size
    offset = jnp.where(offset > cycle_size // 2, offset - cycle_size, offset)
    source_slot = (offset + REACH) * blocks + col_block
    targets = (2 * REACH + 1) * blocks
    pick_source = one_hot_table(source_slot, targets, jnp.bfloat16)
    pick_row = one_hot_table(local_row, blocks, jnp.bfloat16)
    add_row = one_hot_table(local_row, blocks, jnp.float32) * live[:, None]
    add_source = one_hot_table(source_slot, targets, jnp.float32) * live[:, None]
    pieces = []
    for distance in range(-REACH, REACH + 1):
        if distance == 0:
            pieces.append(features)
        else:
            pieces.append(passed_along(features, "node", -distance))
    nearby = jnp.concatenate(pieces, axis=0)
    weight_half = weight.astype(jnp.bfloat16)
    packed = jnp.concatenate([cotangent, weight_half[None]], axis=0)
    packed_all = gathered_along(packed, "feat", 1)
    cotangent_all = packed_all[:blocks]
    weight_all = packed_all[blocks]
    nearby, cotangent_all, weight_all = lax.optimization_barrier((nearby, cotangent_all, weight_all))
    sources = jnp.einsum(
        "ts,sfk->tfk", pick_source, nearby, preferred_element_type=jnp.float32
    ).astype(jnp.bfloat16)
    forward_terms = jnp.einsum(
        "tfk,tjk->tfj", sources, tile_values, preferred_element_type=jnp.float32
    )
    aggregate = jnp.einsum("tb,tfj->bfj", add_row, forward_terms, precision=lax.Precision.HIGHEST)
    aggregate = aggregate.astype(jnp.bfloat16)
    aggregate_all = gathered_along(aggregate, "feat", 1)
    column_start = lax.axis_index("feat") * width_local
    preact = jnp.einsum(
        "bij,io->boj", aggregate_all, weight_all, preferred_element_type=jnp.float32
    )
    activated = lax.dynamic_slice_in_dim(jax.nn.elu(preact), column_start, width_local, 1)
    activated = activated.astype(jnp.bfloat16)
    slope_all = (cotangent_all.astype(jnp.float32) * elu_slope(preact)).astype(jnp.bfloat16)
    node_total = cycle_size * blocks * tile_size
    grad_local = jnp.einsum("bij,boj->io", aggregate, slope_all, preferred_element_type=jnp.float32)
    grad = summed_over(grad_local, "node") * (1.0 / math.sqrt(node_total))
    back_rows = jnp.einsum(
        "io,boj->bij", weight_half, slope_all, preferred_element_type=jnp.float32
    ).astype(jnp.bfloat16)
    back_sources = jnp.einsum(
        "tb,bfj->tfj", pick_row, back_rows, preferred_element_type=jnp.float32
    ).astype(jnp.bfloat16)
    back_terms = jnp.einsum(
        "tfj,tjk->tfk", back_sources, tile_values, preferred_element_type=jnp.float32
    )
    outgoing = jnp.einsum("ts,tfk->sfk", add_source, back_terms, precision=lax.Precision.HIGHEST)
    outgoing = outgoing.reshape(2 * REACH + 1, blocks, width_local, tile_size)
    outgoing, grad = lax.optimization_barrier((outgoing, grad))
    feature_grad = outgoing[REACH]
    for distance in range(-REACH, REACH + 1):
        if distance != 0:
            feature_grad = feature_grad + passed_along(outgoing[distance + REACH], "node", distance)
    new_first = first_decay * first_moment + (1.0 - first_decay) * grad
    new_second = second_decay * second_moment + (1.0 - second_decay) * grad * grad
    new_weight = weight - learn_rate * (new_first / first_fix) / (
        jnp.sqrt(new_second / second_fix) + adam_eps
    )
    return (activated, feature_grad, new_weight, new_first, new_second)


def solution(mesh):
    return jax.shard_map(
        per_device,
        mesh=mesh,
        in_specs=(
            P("node", "feat", None),
            P("node", None, None),
            P("node"),
            P("node"),
            P("node"),
            P("feat", None),
            P("feat", None),
            P("feat", None),
            P("node", "feat", None),
        ),
        out_specs=(
            P("node", "feat", None),
            P("node", "feat", None),
            P("feat", None),
            P("feat", None),
            P("feat", None),
        ),
        check_vma=False,
    )
```

```python
import math

import jax
import jax.numpy as jnp
from jax import lax
from jax.sharding import PartitionSpec as P

REACH = 2


first_decay = 0.9
second_decay = 0.999
learn_rate = 0.05
first_fix = 1.0 - 0.9**10
second_fix = 1.0 - 0.999**10
adam_eps = 1e-08


def passed_along(block, axis, distance):
    devices = range(lax.axis_size(axis))
    route = [((i - distance) % len(devices), i) for i in devices]
    return lax.ppermute(block, axis, route)


def gathered_along(block, axis, dim):
    size = lax.axis_size(axis)
    own = lax.axis_index(axis)
    width = block.shape[dim]
    if size & (size - 1):
        pieces = [(block, own)]
        for step in range(1, size):
            pieces.append((passed_along(block, axis, -step), (own + step) % size))
    else:
        pieces = [(block, own)]
        mask = size // 2
        while mask >= 1:
            held = jnp.stack([piece for piece, _ in pieces])
            got = lax.ppermute(held, axis, [(i, i ^ mask) for i in range(size)])
            pieces = pieces + [(got[k], index ^ mask) for k, (_, index) in enumerate(pieces)]
            mask //= 2
    shape = list(block.shape)
    shape[dim] = size * width
    whole = jnp.zeros(shape, block.dtype)
    for piece, index in pieces:
        whole = lax.dynamic_update_slice_in_dim(whole, piece, index * width, dim)
    return whole


def summed_over(block, axis):
    size = lax.axis_size(axis)
    if size & (size - 1):
        return lax.psum(block, axis)
    mask = 1
    while mask < size:
        block = block + lax.ppermute(block, axis, [(i, i ^ mask) for i in range(size)])
        mask *= 2
    return block


def elu_slope(preact):
    return jnp.where(preact > 0, 1.0, jnp.exp(jnp.minimum(preact, 0.0)))


def one_hot_table(indices, count, dtype):
    return (indices[:, None] == jnp.arange(count)[None, :]).astype(dtype)


def per_device(
    features,
    tile_values,
    tile_row,
    tile_col,
    tile_count,
    weight,
    first_moment,
    second_moment,
    cotangent,
):
    cycle_size = lax.axis_size("node")
    own_node = lax.axis_index("node")
    blocks = features.shape[0]
    width_local = features.shape[1]
    tile_size = features.shape[2]
    slots = tile_values.shape[0]
    live = (jnp.arange(slots) < tile_count[0]).astype(jnp.float32)
    local_row = tile_row - own_node * blocks
    col_owner = tile_col // blocks
    col_block = tile_col % blocks
    offset = (col_owner - own_node) % cycle_size
    offset = jnp.where(offset > cycle_size // 2, offset - cycle_size, offset)
    source_slot = (offset + REACH) * blocks + col_block
    targets = (2 * REACH + 1) * blocks
    pick_source = one_hot_table(source_slot, targets, jnp.bfloat16)
    pick_row = one_hot_table(local_row, blocks, jnp.bfloat16)
    add_row = one_hot_table(local_row, blocks, jnp.float32) * live[:, None]
    add_source = one_hot_table(source_slot, targets, jnp.float32) * live[:, None]
    pieces = []
    for distance in range(-REACH, REACH + 1):
        if distance == 0:
            pieces.append(features)
        else:
            pieces.append(passed_along(features, "node", -distance))
    nearby = jnp.concatenate(pieces, axis=0)
    weight_half = weight.astype(jnp.bfloat16)
    packed = jnp.concatenate([cotangent, weight_half[None]], axis=0)
    packed_all = gathered_along(packed, "feat", 1)
    cotangent_all = packed_all[:blocks]
    weight_all = packed_all[blocks]
    nearby, cotangent_all, weight_all = lax.optimization_barrier((nearby, cotangent_all, weight_all))
    sources = jnp.einsum(
        "ts,sfk->tfk", pick_source, nearby, preferred_element_type=jnp.float32
    ).astype(jnp.bfloat16)
    forward_terms = jnp.einsum(
        "tfk,tjk->tfj", sources, tile_values, preferred_element_type=jnp.float32
    )
    aggregate = jnp.einsum("tb,tfj->bfj", add_row, forward_terms, precision=lax.Precision.HIGH)
    aggregate = aggregate.astype(jnp.bfloat16)
    aggregate_all = gathered_along(aggregate, "feat", 1)
    column_start = lax.axis_index("feat") * width_local
    preact = jnp.einsum(
        "bij,io->boj", aggregate_all, weight_all, preferred_element_type=jnp.float32
    )
    activated = lax.dynamic_slice_in_dim(jax.nn.elu(preact), column_start, width_local, 1)
    activated = activated.astype(jnp.bfloat16)
    slope_all = (cotangent_all.astype(jnp.float32) * elu_slope(preact)).astype(jnp.bfloat16)
    node_total = cycle_size * blocks * tile_size
    grad_local = jnp.einsum("bij,boj->io", aggregate, slope_all, preferred_element_type=jnp.float32)
    grad = summed_over(grad_local, "node") * (1.0 / math.sqrt(node_total))
    back_rows = jnp.einsum(
        "io,boj->bij", weight_half, slope_all, preferred_element_type=jnp.float32
    ).astype(jnp.bfloat16)
    back_sources = jnp.einsum(
        "tb,bfj->tfj", pick_row, back_rows, preferred_element_type=jnp.float32
    ).astype(jnp.bfloat16)
    back_terms = jnp.einsum(
        "tfj,tjk->tfk", back_sources, tile_values, preferred_element_type=jnp.float32
    )
    outgoing = jnp.einsum("ts,tfk->sfk", add_source, back_terms, precision=lax.Precision.HIGH)
    outgoing = outgoing.reshape(2 * REACH + 1, blocks, width_local, tile_size)
    outgoing, grad = lax.optimization_barrier((outgoing, grad))
    feature_grad = outgoing[REACH]
    for distance in range(-REACH, REACH + 1):
        if distance != 0:
            feature_grad = feature_grad + passed_along(outgoing[distance + REACH], "node", distance)
    new_first = first_decay * first_moment + (1.0 - first_decay) * grad
    new_second = second_decay * second_moment + (1.0 - second_decay) * grad * grad
    new_weight = weight - learn_rate * (new_first / first_fix) / (
        jnp.sqrt(new_second / second_fix) + adam_eps
    )
    return (activated, feature_grad, new_weight, new_first, new_second)


def solution(mesh):
    return jax.shard_map(
        per_device,
        mesh=mesh,
        in_specs=(
            P("node", "feat", None),
            P("node", None, None),
            P("node"),
            P("node"),
            P("node"),
            P("feat", None),
            P("feat", None),
            P("feat", None),
            P("node", "feat", None),
        ),
        out_specs=(
            P("node", "feat", None),
            P("node", "feat", None),
            P("feat", None),
            P("feat", None),
            P("feat", None),
        ),
        check_vma=False,
    )
```

```python
import math

import jax
import jax.numpy as jnp
from jax import lax
from jax.sharding import PartitionSpec as P

REACH = 2


first_decay = 0.9
second_decay = 0.999
learn_rate = 0.05
first_fix = 1.0 - 0.9**10
second_fix = 1.0 - 0.999**10
adam_eps = 1e-08


def passed_along(block, axis, distance):
    devices = range(lax.axis_size(axis))
    route = [((i - distance) % len(devices), i) for i in devices]
    return lax.ppermute(block, axis, route)


def gathered_along(block, axis, dim):
    size = lax.axis_size(axis)
    own = lax.axis_index(axis)
    width = block.shape[dim]
    if size & (size - 1):
        pieces = [(block, own)]
        for step in range(1, size):
            pieces.append((passed_along(block, axis, -step), (own + step) % size))
    else:
        pieces = [(block, own)]
        mask = size // 2
        while mask >= 1:
            held = jnp.stack([piece for piece, _ in pieces])
            got = lax.ppermute(held, axis, [(i, i ^ mask) for i in range(size)])
            pieces = pieces + [(got[k], index ^ mask) for k, (_, index) in enumerate(pieces)]
            mask //= 2
    shape = list(block.shape)
    shape[dim] = size * width
    whole = jnp.zeros(shape, block.dtype)
    for piece, index in pieces:
        whole = lax.dynamic_update_slice_in_dim(whole, piece, index * width, dim)
    return whole


def summed_over(block, axis):
    size = lax.axis_size(axis)
    if size & (size - 1):
        return lax.psum(block, axis)
    mask = 1
    while mask < size:
        block = block + lax.ppermute(block, axis, [(i, i ^ mask) for i in range(size)])
        mask *= 2
    return block


def elu_slope(preact):
    return jnp.where(preact > 0, 1.0, jnp.exp(jnp.minimum(preact, 0.0)))


def one_hot_table(indices, count, dtype):
    return (indices[:, None] == jnp.arange(count)[None, :]).astype(dtype)


def per_device(
    features,
    tile_values,
    tile_row,
    tile_col,
    tile_count,
    weight,
    first_moment,
    second_moment,
    cotangent,
):
    cycle_size = lax.axis_size("node")
    own_node = lax.axis_index("node")
    blocks = features.shape[0]
    width_local = features.shape[1]
    tile_size = features.shape[2]
    slots = tile_values.shape[0]
    live = (jnp.arange(slots) < tile_count[0]).astype(jnp.float32)
    local_row = tile_row - own_node * blocks
    col_owner = tile_col // blocks
    col_block = tile_col % blocks
    offset = (col_owner - own_node) % cycle_size
    offset = jnp.where(offset > cycle_size // 2, offset - cycle_size, offset)
    source_slot = (offset + REACH) * blocks + col_block
    targets = (2 * REACH + 1) * blocks
    pick_source = one_hot_table(source_slot, targets, jnp.bfloat16)
    pick_row = one_hot_table(local_row, blocks, jnp.bfloat16)
    add_row = one_hot_table(local_row, blocks, jnp.float32) * live[:, None]
    add_source = one_hot_table(source_slot, targets, jnp.float32) * live[:, None]
    pieces = []
    for distance in range(-REACH, REACH + 1):
        if distance == 0:
            pieces.append(features)
        else:
            pieces.append(passed_along(features, "node", -distance))
    nearby = jnp.concatenate(pieces, axis=0)
    weight_half = weight.astype(jnp.bfloat16)
    packed = jnp.concatenate([cotangent, weight_half[None]], axis=0)
    packed_all = gathered_along(packed, "feat", 1)
    cotangent_all = packed_all[:blocks]
    weight_all = packed_all[blocks]
    nearby, cotangent_all, weight_all = lax.optimization_barrier((nearby, cotangent_all, weight_all))
    sources = jnp.einsum(
        "ts,sfk->tfk", pick_source, nearby, preferred_element_type=jnp.float32
    ).astype(jnp.bfloat16)
    forward_terms = jnp.einsum(
        "tfk,tjk->tfj", sources, tile_values, preferred_element_type=jnp.float32
    )
    aggregate = jnp.einsum("tb,tfj->bfj", add_row, forward_terms, precision=lax.Precision.HIGH)
    aggregate = aggregate.astype(jnp.bfloat16)
    aggregate_all = gathered_along(aggregate, "feat", 1)
    column_start = lax.axis_index("feat") * width_local
    preact = jnp.einsum(
        "bij,io->boj", aggregate_all, weight_all, preferred_element_type=jnp.float32
    )
    activated = lax.dynamic_slice_in_dim(jax.nn.elu(preact), column_start, width_local, 1)
    activated = activated.astype(jnp.bfloat16)
    slope_all = (cotangent_all.astype(jnp.float32) * elu_slope(preact)).astype(jnp.bfloat16)
    node_total = cycle_size * blocks * tile_size
    grad_local = jnp.einsum("bij,boj->io", aggregate, slope_all, preferred_element_type=jnp.float32)
    grad = summed_over(grad_local, "node") * (1.0 / math.sqrt(node_total))
    back_rows = jnp.einsum(
        "io,boj->bij", weight_half, slope_all, preferred_element_type=jnp.float32
    ).astype(jnp.bfloat16)
    back_sources = jnp.einsum(
        "tb,bfj->tfj", pick_row, back_rows, preferred_element_type=jnp.float32
    ).astype(jnp.bfloat16)
    back_terms = jnp.einsum(
        "tfj,tjk->tfk", back_sources, tile_values, preferred_element_type=jnp.float32
    )
    outgoing = jnp.einsum("ts,tfk->sfk", add_source, back_terms, precision=lax.Precision.HIGH)
    outgoing = outgoing.reshape(2 * REACH + 1, blocks, width_local, tile_size)
    outgoing, grad = lax.optimization_barrier((outgoing, grad))
    feature_grad = outgoing[REACH]
    for distance in range(-REACH, REACH + 1):
        if distance != 0:
            sent = outgoing[distance + REACH].astype(jnp.bfloat16)
            feature_grad = feature_grad + passed_along(sent, "node", distance).astype(jnp.float32)
    new_first = first_decay * first_moment + (1.0 - first_decay) * grad
    new_second = second_decay * second_moment + (1.0 - second_decay) * grad * grad
    new_weight = weight - learn_rate * (new_first / first_fix) / (
        jnp.sqrt(new_second / second_fix) + adam_eps
    )
    return (activated, feature_grad, new_weight, new_first, new_second)


def solution(mesh):
    return jax.shard_map(
        per_device,
        mesh=mesh,
        in_specs=(
            P("node", "feat", None),
            P("node", None, None),
            P("node"),
            P("node"),
            P("node"),
            P("feat", None),
            P("feat", None),
            P("feat", None),
            P("node", "feat", None),
        ),
        out_specs=(
            P("node", "feat", None),
            P("node", "feat", None),
            P("feat", None),
            P("feat", None),
            P("feat", None),
        ),
        check_vma=False,
    )
```

```python
import math

import jax
import jax.numpy as jnp
from jax import lax
from jax.sharding import PartitionSpec as P

REACH = 2


first_decay = 0.9
second_decay = 0.999
learn_rate = 0.05
first_fix = 1.0 - 0.9**10
second_fix = 1.0 - 0.999**10
adam_eps = 1e-08


def passed_along(block, axis, distance):
    devices = range(lax.axis_size(axis))
    route = [((i - distance) % len(devices), i) for i in devices]
    return lax.ppermute(block, axis, route)


def gathered_along(block, axis, dim):
    size = lax.axis_size(axis)
    own = lax.axis_index(axis)
    width = block.shape[dim]
    if size & (size - 1):
        pieces = [(block, own)]
        for step in range(1, size):
            pieces.append((passed_along(block, axis, -step), (own + step) % size))
    else:
        pieces = [(block, own)]
        mask = size // 2
        while mask >= 1:
            held = jnp.stack([piece for piece, _ in pieces])
            got = lax.ppermute(held, axis, [(i, i ^ mask) for i in range(size)])
            pieces = pieces + [(got[k], index ^ mask) for k, (_, index) in enumerate(pieces)]
            mask //= 2
    shape = list(block.shape)
    shape[dim] = size * width
    whole = jnp.zeros(shape, block.dtype)
    for piece, index in pieces:
        whole = lax.dynamic_update_slice_in_dim(whole, piece, index * width, dim)
    return whole


def summed_over(block, axis):
    size = lax.axis_size(axis)
    if size & (size - 1):
        return lax.psum(block, axis)
    mask = 1
    while mask < size:
        block = block + lax.ppermute(block, axis, [(i, i ^ mask) for i in range(size)])
        mask *= 2
    return block


def summed_by_table(table, terms, spec):
    high = terms.astype(jnp.bfloat16)
    low = (terms - high.astype(jnp.float32)).astype(jnp.bfloat16)
    both = jnp.concatenate([high, low], axis=0)
    doubled = jnp.concatenate([table, table], axis=0).astype(jnp.bfloat16)
    return jnp.einsum(spec, doubled, both, preferred_element_type=jnp.float32)


def elu_slope(preact):
    return jnp.where(preact > 0, 1.0, jnp.exp(jnp.minimum(preact, 0.0)))


def one_hot_table(indices, count, dtype):
    return (indices[:, None] == jnp.arange(count)[None, :]).astype(dtype)


def per_device(
    features,
    tile_values,
    tile_row,
    tile_col,
    tile_count,
    weight,
    first_moment,
    second_moment,
    cotangent,
):
    cycle_size = lax.axis_size("node")
    own_node = lax.axis_index("node")
    blocks = features.shape[0]
    width_local = features.shape[1]
    tile_size = features.shape[2]
    slots = tile_values.shape[0]
    live = (jnp.arange(slots) < tile_count[0]).astype(jnp.float32)
    local_row = tile_row - own_node * blocks
    col_owner = tile_col // blocks
    col_block = tile_col % blocks
    offset = (col_owner - own_node) % cycle_size
    offset = jnp.where(offset > cycle_size // 2, offset - cycle_size, offset)
    source_slot = (offset + REACH) * blocks + col_block
    targets = (2 * REACH + 1) * blocks
    pick_source = one_hot_table(source_slot, targets, jnp.bfloat16)
    pick_row = one_hot_table(local_row, blocks, jnp.bfloat16)
    add_row = one_hot_table(local_row, blocks, jnp.float32) * live[:, None]
    add_source = one_hot_table(source_slot, targets, jnp.float32) * live[:, None]
    pieces = []
    for distance in range(-REACH, REACH + 1):
        if distance == 0:
            pieces.append(features)
        else:
            pieces.append(passed_along(features, "node", -distance))
    nearby = jnp.concatenate(pieces, axis=0)
    weight_half = weight.astype(jnp.bfloat16)
    packed = jnp.concatenate([cotangent, weight_half[None]], axis=0)
    packed_all = gathered_along(packed, "feat", 1)
    cotangent_all = packed_all[:blocks]
    weight_all = packed_all[blocks]
    nearby, cotangent_all, weight_all = lax.optimization_barrier((nearby, cotangent_all, weight_all))
    sources = jnp.einsum(
        "ts,sfk->tfk", pick_source, nearby, preferred_element_type=jnp.float32
    ).astype(jnp.bfloat16)
    forward_terms = jnp.einsum(
        "tfk,tjk->tfj", sources, tile_values, preferred_element_type=jnp.float32
    )
    aggregate = summed_by_table(add_row, forward_terms, "tb,tfj->bfj")
    aggregate = aggregate.astype(jnp.bfloat16)
    aggregate_all = gathered_along(aggregate, "feat", 1)
    column_start = lax.axis_index("feat") * width_local
    preact = jnp.einsum(
        "bij,io->boj", aggregate_all, weight_all, preferred_element_type=jnp.float32
    )
    activated = lax.dynamic_slice_in_dim(jax.nn.elu(preact), column_start, width_local, 1)
    activated = activated.astype(jnp.bfloat16)
    slope_all = (cotangent_all.astype(jnp.float32) * elu_slope(preact)).astype(jnp.bfloat16)
    node_total = cycle_size * blocks * tile_size
    grad_local = jnp.einsum("bij,boj->io", aggregate, slope_all, preferred_element_type=jnp.float32)
    grad = summed_over(grad_local, "node") * (1.0 / math.sqrt(node_total))
    back_rows = jnp.einsum(
        "io,boj->bij", weight_half, slope_all, preferred_element_type=jnp.float32
    ).astype(jnp.bfloat16)
    back_sources = jnp.einsum(
        "tb,bfj->tfj", pick_row, back_rows, preferred_element_type=jnp.float32
    ).astype(jnp.bfloat16)
    back_terms = jnp.einsum(
        "tfj,tjk->tfk", back_sources, tile_values, preferred_element_type=jnp.float32
    )
    outgoing = summed_by_table(add_source, back_terms, "ts,tfk->sfk")
    outgoing = outgoing.reshape(2 * REACH + 1, blocks, width_local, tile_size)
    outgoing, grad = lax.optimization_barrier((outgoing, grad))
    feature_grad = outgoing[REACH]
    for distance in range(-REACH, REACH + 1):
        if distance != 0:
            sent = outgoing[distance + REACH].astype(jnp.bfloat16)
            feature_grad = feature_grad + passed_along(sent, "node", distance).astype(jnp.float32)
    new_first = first_decay * first_moment + (1.0 - first_decay) * grad
    new_second = second_decay * second_moment + (1.0 - second_decay) * grad * grad
    new_weight = weight - learn_rate * (new_first / first_fix) / (
        jnp.sqrt(new_second / second_fix) + adam_eps
    )
    return (activated, feature_grad, new_weight, new_first, new_second)


def solution(mesh):
    return jax.shard_map(
        per_device,
        mesh=mesh,
        in_specs=(
            P("node", "feat", None),
            P("node", None, None),
            P("node"),
            P("node"),
            P("node"),
            P("feat", None),
            P("feat", None),
            P("feat", None),
            P("node", "feat", None),
        ),
        out_specs=(
            P("node", "feat", None),
            P("node", "feat", None),
            P("feat", None),
            P("feat", None),
            P("feat", None),
        ),
        check_vma=False,
    )
```

```python
import math

import jax
import jax.numpy as jnp
from jax import lax
from jax.sharding import PartitionSpec as P

REACH = 2


first_decay = 0.9
second_decay = 0.999
learn_rate = 0.05
first_fix = 1.0 - 0.9**10
second_fix = 1.0 - 0.999**10
adam_eps = 1e-08


def passed_along(block, axis, distance):
    devices = range(lax.axis_size(axis))
    route = [((i - distance) % len(devices), i) for i in devices]
    return lax.ppermute(block, axis, route)


def gathered_along(block, axis, dim):
    size = lax.axis_size(axis)
    own = lax.axis_index(axis)
    width = block.shape[dim]
    if size & (size - 1):
        pieces = [(block, own)]
        for step in range(1, size):
            pieces.append((passed_along(block, axis, -step), (own + step) % size))
    else:
        pieces = [(block, own)]
        mask = size // 2
        while mask >= 1:
            held = jnp.stack([piece for piece, _ in pieces])
            got = lax.ppermute(held, axis, [(i, i ^ mask) for i in range(size)])
            pieces = pieces + [(got[k], index ^ mask) for k, (_, index) in enumerate(pieces)]
            mask //= 2
    shape = list(block.shape)
    shape[dim] = size * width
    whole = jnp.zeros(shape, block.dtype)
    for piece, index in pieces:
        whole = lax.dynamic_update_slice_in_dim(whole, piece, index * width, dim)
    return whole


def summed_over(block, axis):
    size = lax.axis_size(axis)
    if size & (size - 1):
        return lax.psum(block, axis)
    mask = 1
    while mask < size:
        block = block + lax.ppermute(block, axis, [(i, i ^ mask) for i in range(size)])
        mask *= 2
    return block


def summed_by_table(table, terms, spec):
    rounded = lax.reduce_precision(terms, exponent_bits=8, mantissa_bits=7)
    high = rounded.astype(jnp.bfloat16)
    low = (terms - rounded).astype(jnp.bfloat16)
    both = jnp.concatenate([high, low], axis=0)
    doubled = jnp.concatenate([table, table], axis=0).astype(jnp.bfloat16)
    return jnp.einsum(spec, doubled, both, preferred_element_type=jnp.float32)


def elu_slope(preact):
    return jnp.where(preact > 0, 1.0, jnp.exp(jnp.minimum(preact, 0.0)))


def one_hot_table(indices, count, dtype):
    return (indices[:, None] == jnp.arange(count)[None, :]).astype(dtype)


def per_device(
    features,
    tile_values,
    tile_row,
    tile_col,
    tile_count,
    weight,
    first_moment,
    second_moment,
    cotangent,
):
    cycle_size = lax.axis_size("node")
    own_node = lax.axis_index("node")
    blocks = features.shape[0]
    width_local = features.shape[1]
    tile_size = features.shape[2]
    slots = tile_values.shape[0]
    live = (jnp.arange(slots) < tile_count[0]).astype(jnp.float32)
    local_row = tile_row - own_node * blocks
    col_owner = tile_col // blocks
    col_block = tile_col % blocks
    offset = (col_owner - own_node) % cycle_size
    offset = jnp.where(offset > cycle_size // 2, offset - cycle_size, offset)
    source_slot = (offset + REACH) * blocks + col_block
    targets = (2 * REACH + 1) * blocks
    pick_source = one_hot_table(source_slot, targets, jnp.bfloat16)
    pick_row = one_hot_table(local_row, blocks, jnp.bfloat16)
    add_row = one_hot_table(local_row, blocks, jnp.float32) * live[:, None]
    add_source = one_hot_table(source_slot, targets, jnp.float32) * live[:, None]
    pieces = []
    for distance in range(-REACH, REACH + 1):
        if distance == 0:
            pieces.append(features)
        else:
            pieces.append(passed_along(features, "node", -distance))
    nearby = jnp.concatenate(pieces, axis=0)
    weight_half = weight.astype(jnp.bfloat16)
    packed = jnp.concatenate([cotangent, weight_half[None]], axis=0)
    packed_all = gathered_along(packed, "feat", 1)
    cotangent_all = packed_all[:blocks]
    weight_all = packed_all[blocks]
    nearby, cotangent_all, weight_all = lax.optimization_barrier((nearby, cotangent_all, weight_all))
    sources = jnp.einsum(
        "ts,sfk->tfk", pick_source, nearby, preferred_element_type=jnp.float32
    ).astype(jnp.bfloat16)
    forward_terms = jnp.einsum(
        "tfk,tjk->tfj", sources, tile_values, preferred_element_type=jnp.float32
    )
    aggregate = summed_by_table(add_row, forward_terms, "tb,tfj->bfj")
    aggregate = aggregate.astype(jnp.bfloat16)
    aggregate_all = gathered_along(aggregate, "feat", 1)
    column_start = lax.axis_index("feat") * width_local
    preact = jnp.einsum(
        "bij,io->boj", aggregate_all, weight_all, preferred_element_type=jnp.float32
    )
    activated = lax.dynamic_slice_in_dim(jax.nn.elu(preact), column_start, width_local, 1)
    activated = activated.astype(jnp.bfloat16)
    slope_all = (cotangent_all.astype(jnp.float32) * elu_slope(preact)).astype(jnp.bfloat16)
    node_total = cycle_size * blocks * tile_size
    grad_local = jnp.einsum("bij,boj->io", aggregate, slope_all, preferred_element_type=jnp.float32)
    grad = summed_over(grad_local, "node") * (1.0 / math.sqrt(node_total))
    back_rows = jnp.einsum(
        "io,boj->bij", weight_half, slope_all, preferred_element_type=jnp.float32
    ).astype(jnp.bfloat16)
    back_sources = jnp.einsum(
        "tb,bfj->tfj", pick_row, back_rows, preferred_element_type=jnp.float32
    ).astype(jnp.bfloat16)
    back_terms = jnp.einsum(
        "tfj,tjk->tfk", back_sources, tile_values, preferred_element_type=jnp.float32
    )
    outgoing = summed_by_table(add_source, back_terms, "ts,tfk->sfk")
    outgoing = outgoing.reshape(2 * REACH + 1, blocks, width_local, tile_size)
    outgoing, grad = lax.optimization_barrier((outgoing, grad))
    feature_grad = outgoing[REACH]
    for distance in range(-REACH, REACH + 1):
        if distance != 0:
            sent = outgoing[distance + REACH].astype(jnp.bfloat16)
            feature_grad = feature_grad + passed_along(sent, "node", distance).astype(jnp.float32)
    new_first = first_decay * first_moment + (1.0 - first_decay) * grad
    new_second = second_decay * second_moment + (1.0 - second_decay) * grad * grad
    new_weight = weight - learn_rate * (new_first / first_fix) / (
        jnp.sqrt(new_second / second_fix) + adam_eps
    )
    return (activated, feature_grad, new_weight, new_first, new_second)


def solution(mesh):
    return jax.shard_map(
        per_device,
        mesh=mesh,
        in_specs=(
            P("node", "feat", None),
            P("node", None, None),
            P("node"),
            P("node"),
            P("node"),
            P("feat", None),
            P("feat", None),
            P("feat", None),
            P("node", "feat", None),
        ),
        out_specs=(
            P("node", "feat", None),
            P("node", "feat", None),
            P("feat", None),
            P("feat", None),
            P("feat", None),
        ),
        check_vma=False,
    )
```

```python
import math

import jax
import jax.numpy as jnp
from jax import lax
from jax.sharding import PartitionSpec as P

REACH = 2


first_decay = 0.9
second_decay = 0.999
learn_rate = 0.05
first_fix = 1.0 - 0.9**10
second_fix = 1.0 - 0.999**10
adam_eps = 1e-08


def passed_along(block, axis, distance):
    devices = range(lax.axis_size(axis))
    route = [((i - distance) % len(devices), i) for i in devices]
    return lax.ppermute(block, axis, route)


def gathered_along(block, axis, dim):
    size = lax.axis_size(axis)
    own = lax.axis_index(axis)
    width = block.shape[dim]
    if size & (size - 1):
        pieces = [(block, own)]
        for step in range(1, size):
            pieces.append((passed_along(block, axis, -step), (own + step) % size))
    else:
        pieces = [(block, own)]
        mask = size // 2
        while mask >= 1:
            held = jnp.stack([piece for piece, _ in pieces])
            got = lax.ppermute(held, axis, [(i, i ^ mask) for i in range(size)])
            pieces = pieces + [(got[k], index ^ mask) for k, (_, index) in enumerate(pieces)]
            mask //= 2
    shape = list(block.shape)
    shape[dim] = size * width
    whole = jnp.zeros(shape, block.dtype)
    for piece, index in pieces:
        whole = lax.dynamic_update_slice_in_dim(whole, piece, index * width, dim)
    return whole


def summed_over(block, axis):
    size = lax.axis_size(axis)
    if size & (size - 1):
        return lax.psum(block, axis)
    mask = 1
    while mask < size:
        block = block + lax.ppermute(block, axis, [(i, i ^ mask) for i in range(size)])
        mask *= 2
    return block


def summed_by_table(table, terms, spec):
    rounded = lax.reduce_precision(terms, exponent_bits=8, mantissa_bits=7)
    high = rounded.astype(jnp.bfloat16)
    low = (terms - rounded).astype(jnp.bfloat16)
    both = jnp.concatenate([high, low], axis=0)
    doubled = jnp.concatenate([table, table], axis=0).astype(jnp.bfloat16)
    return jnp.einsum(spec, doubled, both, preferred_element_type=jnp.float32)


def elu_slope(preact):
    return jnp.where(preact > 0, 1.0, jnp.exp(jnp.minimum(preact, 0.0)))


def one_hot_table(indices, count, dtype):
    return (indices[:, None] == jnp.arange(count)[None, :]).astype(dtype)


def per_device(
    features,
    tile_values,
    tile_row,
    tile_col,
    tile_count,
    weight,
    first_moment,
    second_moment,
    cotangent,
):
    cycle_size = lax.axis_size("node")
    own_node = lax.axis_index("node")
    blocks = features.shape[0]
    width_local = features.shape[1]
    tile_size = features.shape[2]
    slots = tile_values.shape[0]
    live = (jnp.arange(slots) < tile_count[0]).astype(jnp.float32)
    local_row = tile_row - own_node * blocks
    col_owner = tile_col // blocks
    col_block = tile_col % blocks
    offset = (col_owner - own_node) % cycle_size
    offset = jnp.where(offset > cycle_size // 2, offset - cycle_size, offset)
    source_slot = (offset + REACH) * blocks + col_block
    targets = (2 * REACH + 1) * blocks
    pick_source = one_hot_table(source_slot, targets, jnp.bfloat16)
    pick_row = one_hot_table(local_row, blocks, jnp.bfloat16)
    add_row = one_hot_table(local_row, blocks, jnp.float32) * live[:, None]
    add_source = one_hot_table(source_slot, targets, jnp.float32) * live[:, None]
    pieces = []
    for distance in range(-REACH, REACH + 1):
        if distance == 0:
            pieces.append(features)
        else:
            pieces.append(passed_along(features, "node", -distance))
    nearby = jnp.concatenate(pieces, axis=0)
    weight_half = weight.astype(jnp.bfloat16)
    packed = jnp.concatenate([cotangent, weight_half[None]], axis=0)
    packed_all = gathered_along(packed, "feat", 1)
    cotangent_all = packed_all[:blocks]
    weight_all = packed_all[blocks]
    nearby, cotangent_all, weight_all = lax.optimization_barrier((nearby, cotangent_all, weight_all))
    sources = jnp.einsum(
        "ts,sfk->tfk", pick_source, nearby, preferred_element_type=jnp.float32
    ).astype(jnp.bfloat16)
    forward_terms = jnp.einsum(
        "tfk,tjk->tfj", sources, tile_values, preferred_element_type=jnp.float32
    )
    aggregate = summed_by_table(add_row, forward_terms, "tb,tfj->bfj")
    aggregate = aggregate.astype(jnp.bfloat16)
    aggregate_all = gathered_along(aggregate, "feat", 1)
    column_start = lax.axis_index("feat") * width_local
    preact = jnp.einsum(
        "bij,io->boj", aggregate_all, weight_all, preferred_element_type=jnp.float32
    )
    activated = lax.dynamic_slice_in_dim(jax.nn.elu(preact), column_start, width_local, 1)
    activated = activated.astype(jnp.bfloat16)
    slope_all = (cotangent_all.astype(jnp.float32) * elu_slope(preact)).astype(jnp.bfloat16)
    node_total = cycle_size * blocks * tile_size
    grad_local = jnp.einsum("bij,boj->io", aggregate, slope_all, preferred_element_type=jnp.float32)
    grad = summed_over(grad_local, "node") * (1.0 / math.sqrt(node_total))
    back_rows = jnp.einsum(
        "io,boj->bij", weight_half, slope_all, preferred_element_type=jnp.float32
    ).astype(jnp.bfloat16)
    back_sources = jnp.einsum(
        "tb,bfj->tfj", pick_row, back_rows, preferred_element_type=jnp.float32
    ).astype(jnp.bfloat16)
    back_terms = jnp.einsum(
        "tfj,tjk->tfk", back_sources, tile_values, preferred_element_type=jnp.float32
    )
    outgoing = summed_by_table(add_source, back_terms, "ts,tfk->sfk")
    outgoing = outgoing.reshape(2 * REACH + 1, blocks, width_local, tile_size)
    feature_grad = outgoing[REACH]
    for distance in range(-REACH, REACH + 1):
        if distance != 0:
            sent = outgoing[distance + REACH].astype(jnp.bfloat16)
            feature_grad = feature_grad + passed_along(sent, "node", distance).astype(jnp.float32)
    new_first = first_decay * first_moment + (1.0 - first_decay) * grad
    new_second = second_decay * second_moment + (1.0 - second_decay) * grad * grad
    new_weight = weight - learn_rate * (new_first / first_fix) / (
        jnp.sqrt(new_second / second_fix) + adam_eps
    )
    return (activated, feature_grad, new_weight, new_first, new_second)


def solution(mesh):
    return jax.shard_map(
        per_device,
        mesh=mesh,
        in_specs=(
            P("node", "feat", None),
            P("node", None, None),
            P("node"),
            P("node"),
            P("node"),
            P("feat", None),
            P("feat", None),
            P("feat", None),
            P("node", "feat", None),
        ),
        out_specs=(
            P("node", "feat", None),
            P("node", "feat", None),
            P("feat", None),
            P("feat", None),
            P("feat", None),
        ),
        check_vma=False,
    )
```

```python
import math

import jax
import jax.numpy as jnp
from jax import lax
from jax.sharding import PartitionSpec as P

REACH = 2


first_decay = 0.9
second_decay = 0.999
learn_rate = 0.05
first_fix = 1.0 - 0.9**10
second_fix = 1.0 - 0.999**10
adam_eps = 1e-08


def passed_along(block, axis, distance):
    devices = range(lax.axis_size(axis))
    route = [((i - distance) % len(devices), i) for i in devices]
    return lax.ppermute(block, axis, route)


def gathered_along(block, axis, dim):
    size = lax.axis_size(axis)
    own = lax.axis_index(axis)
    width = block.shape[dim]
    if size & (size - 1):
        pieces = [(block, own)]
        for step in range(1, size):
            pieces.append((passed_along(block, axis, -step), (own + step) % size))
    else:
        pieces = [(block, own)]
        mask = size // 2
        while mask >= 1:
            held = jnp.stack([piece for piece, _ in pieces])
            got = lax.ppermute(held, axis, [(i, i ^ mask) for i in range(size)])
            pieces = pieces + [(got[k], index ^ mask) for k, (_, index) in enumerate(pieces)]
            mask //= 2
    shape = list(block.shape)
    shape[dim] = size * width
    whole = jnp.zeros(shape, block.dtype)
    for piece, index in pieces:
        whole = lax.dynamic_update_slice_in_dim(whole, piece, index * width, dim)
    return whole


def summed_over(block, axis):
    size = lax.axis_size(axis)
    if size & (size - 1):
        return lax.psum(block, axis)
    mask = 1
    while mask < size:
        block = block + lax.ppermute(block, axis, [(i, i ^ mask) for i in range(size)])
        mask *= 2
    return block


def summed_by_table(table, terms, spec):
    rounded = lax.reduce_precision(terms, exponent_bits=8, mantissa_bits=7)
    high = rounded.astype(jnp.bfloat16)
    low = (terms - rounded).astype(jnp.bfloat16)
    both = jnp.concatenate([high, low], axis=0)
    doubled = jnp.concatenate([table, table], axis=0).astype(jnp.bfloat16)
    return jnp.einsum(spec, doubled, both, preferred_element_type=jnp.float32)


def elu_slope(preact):
    return jnp.where(preact > 0, 1.0, jnp.exp(jnp.minimum(preact, 0.0)))


def one_hot_table(indices, count, dtype):
    return (indices[:, None] == jnp.arange(count)[None, :]).astype(dtype)


def per_device(
    features,
    tile_values,
    tile_row,
    tile_col,
    tile_count,
    weight,
    first_moment,
    second_moment,
    cotangent,
):
    cycle_size = lax.axis_size("node")
    own_node = lax.axis_index("node")
    blocks = features.shape[0]
    width_local = features.shape[1]
    tile_size = features.shape[2]
    slots = tile_values.shape[0]
    live = (jnp.arange(slots) < tile_count[0]).astype(jnp.float32)
    local_row = tile_row - own_node * blocks
    col_owner = tile_col // blocks
    col_block = tile_col % blocks
    offset = (col_owner - own_node) % cycle_size
    offset = jnp.where(offset > cycle_size // 2, offset - cycle_size, offset)
    source_slot = (offset + REACH) * blocks + col_block
    targets = (2 * REACH + 1) * blocks
    pick_source = one_hot_table(source_slot, targets, jnp.bfloat16)
    pick_row = one_hot_table(local_row, blocks, jnp.bfloat16)
    add_row = one_hot_table(local_row, blocks, jnp.float32) * live[:, None]
    add_source = one_hot_table(source_slot, targets, jnp.float32) * live[:, None]
    pieces = []
    for distance in range(-REACH, REACH + 1):
        if distance == 0:
            pieces.append(features)
        else:
            pieces.append(passed_along(features, "node", -distance))
    nearby = jnp.concatenate(pieces, axis=0)
    weight_half = weight.astype(jnp.bfloat16)
    packed = jnp.concatenate([cotangent, weight_half[None]], axis=0)
    packed_all = gathered_along(packed, "feat", 1)
    cotangent_all = packed_all[:blocks]
    weight_all = packed_all[blocks]
    nearby, cotangent_all, weight_all = lax.optimization_barrier((nearby, cotangent_all, weight_all))
    sources = jnp.einsum(
        "ts,sfk->tfk", pick_source, nearby, preferred_element_type=jnp.float32
    ).astype(jnp.bfloat16)
    forward_terms = jnp.einsum(
        "tjk,tfk->tjf", tile_values, sources, preferred_element_type=jnp.float32
    )
    aggregate = summed_by_table(add_row, forward_terms, "tb,tjf->bfj")
    aggregate = aggregate.astype(jnp.bfloat16)
    aggregate_all = gathered_along(aggregate, "feat", 1)
    column_start = lax.axis_index("feat") * width_local
    preact = jnp.einsum(
        "bij,io->boj", aggregate_all, weight_all, preferred_element_type=jnp.float32
    )
    activated = lax.dynamic_slice_in_dim(jax.nn.elu(preact), column_start, width_local, 1)
    activated = activated.astype(jnp.bfloat16)
    slope_all = (cotangent_all.astype(jnp.float32) * elu_slope(preact)).astype(jnp.bfloat16)
    node_total = cycle_size * blocks * tile_size
    grad_local = jnp.einsum("bij,boj->io", aggregate, slope_all, preferred_element_type=jnp.float32)
    grad = summed_over(grad_local, "node") * (1.0 / math.sqrt(node_total))
    back_rows = jnp.einsum(
        "io,boj->bij", weight_half, slope_all, preferred_element_type=jnp.float32
    ).astype(jnp.bfloat16)
    back_sources = jnp.einsum(
        "tb,bfj->tfj", pick_row, back_rows, preferred_element_type=jnp.float32
    ).astype(jnp.bfloat16)
    back_terms = jnp.einsum(
        "tfj,tjk->tfk", back_sources, tile_values, preferred_element_type=jnp.float32
    )
    outgoing = summed_by_table(add_source, back_terms, "ts,tfk->sfk")
    outgoing = outgoing.reshape(2 * REACH + 1, blocks, width_local, tile_size)
    feature_grad = outgoing[REACH]
    for distance in range(-REACH, REACH + 1):
        if distance != 0:
            sent = outgoing[distance + REACH].astype(jnp.bfloat16)
            feature_grad = feature_grad + passed_along(sent, "node", distance).astype(jnp.float32)
    new_first = first_decay * first_moment + (1.0 - first_decay) * grad
    new_second = second_decay * second_moment + (1.0 - second_decay) * grad * grad
    new_weight = weight - learn_rate * (new_first / first_fix) / (
        jnp.sqrt(new_second / second_fix) + adam_eps
    )
    return (activated, feature_grad, new_weight, new_first, new_second)


def solution(mesh):
    return jax.shard_map(
        per_device,
        mesh=mesh,
        in_specs=(
            P("node", "feat", None),
            P("node", None, None),
            P("node"),
            P("node"),
            P("node"),
            P("feat", None),
            P("feat", None),
            P("feat", None),
            P("node", "feat", None),
        ),
        out_specs=(
            P("node", "feat", None),
            P("node", "feat", None),
            P("feat", None),
            P("feat", None),
            P("feat", None),
        ),
        check_vma=False,
    )
```

```python
import math

import jax
import jax.numpy as jnp
from jax import lax
from jax.sharding import PartitionSpec as P

REACH = 2


first_decay = 0.9
second_decay = 0.999
learn_rate = 0.05
first_fix = 1.0 - 0.9**10
second_fix = 1.0 - 0.999**10
adam_eps = 1e-08


def passed_along(block, axis, distance):
    devices = range(lax.axis_size(axis))
    route = [((i - distance) % len(devices), i) for i in devices]
    return lax.ppermute(block, axis, route)


def gathered_along(block, axis, dim):
    size = lax.axis_size(axis)
    own = lax.axis_index(axis)
    width = block.shape[dim]
    if size & (size - 1):
        pieces = [(block, own)]
        for step in range(1, size):
            pieces.append((passed_along(block, axis, -step), (own + step) % size))
    else:
        pieces = [(block, own)]
        mask = size // 2
        while mask >= 1:
            held = jnp.stack([piece for piece, _ in pieces])
            got = lax.ppermute(held, axis, [(i, i ^ mask) for i in range(size)])
            pieces = pieces + [(got[k], index ^ mask) for k, (_, index) in enumerate(pieces)]
            mask //= 2
    shape = list(block.shape)
    shape[dim] = size * width
    whole = jnp.zeros(shape, block.dtype)
    for piece, index in pieces:
        whole = lax.dynamic_update_slice_in_dim(whole, piece, index * width, dim)
    return whole


def summed_over(block, axis):
    size = lax.axis_size(axis)
    if size & (size - 1):
        return lax.psum(block, axis)
    own = lax.axis_index(axis)
    stride = 1
    while stride < size:
        if stride * 4 <= size:
            held = [block]
            for k in (1, 2, 3):
                route = [(i, i ^ (k * stride)) for i in range(size)]
                held.append(lax.ppermute(block, axis, route))
            held = jnp.stack(held)
            member = (own // stride) % 4
            ordered = [held[m ^ member] for m in range(4)]
            block = (ordered[0] + ordered[1]) + (ordered[2] + ordered[3])
            stride *= 4
        else:
            block = block + lax.ppermute(block, axis, [(i, i ^ stride) for i in range(size)])
            stride *= 2
    return block


def summed_by_table(table, terms, spec):
    rounded = lax.reduce_precision(terms, exponent_bits=8, mantissa_bits=7)
    high = rounded.astype(jnp.bfloat16)
    low = (terms - rounded).astype(jnp.bfloat16)
    both = jnp.concatenate([high, low], axis=0)
    doubled = jnp.concatenate([table, table], axis=0).astype(jnp.bfloat16)
    return jnp.einsum(spec, doubled, both, preferred_element_type=jnp.float32)


def elu_slope(preact):
    return jnp.where(preact > 0, 1.0, jnp.exp(jnp.minimum(preact, 0.0)))


def one_hot_table(indices, count, dtype):
    return (indices[:, None] == jnp.arange(count)[None, :]).astype(dtype)


def per_device(
    features,
    tile_values,
    tile_row,
    tile_col,
    tile_count,
    weight,
    first_moment,
    second_moment,
    cotangent,
):
    cycle_size = lax.axis_size("node")
    own_node = lax.axis_index("node")
    blocks = features.shape[0]
    width_local = features.shape[1]
    tile_size = features.shape[2]
    slots = tile_values.shape[0]
    live = (jnp.arange(slots) < tile_count[0]).astype(jnp.float32)
    local_row = tile_row - own_node * blocks
    col_owner = tile_col // blocks
    col_block = tile_col % blocks
    offset = (col_owner - own_node) % cycle_size
    offset = jnp.where(offset > cycle_size // 2, offset - cycle_size, offset)
    source_slot = (offset + REACH) * blocks + col_block
    targets = (2 * REACH + 1) * blocks
    pick_source = one_hot_table(source_slot, targets, jnp.bfloat16)
    pick_row = one_hot_table(local_row, blocks, jnp.bfloat16)
    add_row = one_hot_table(local_row, blocks, jnp.float32) * live[:, None]
    add_source = one_hot_table(source_slot, targets, jnp.float32) * live[:, None]
    pieces = []
    for distance in range(-REACH, REACH + 1):
        if distance == 0:
            pieces.append(features)
        else:
            pieces.append(passed_along(features, "node", -distance))
    nearby = jnp.concatenate(pieces, axis=0)
    weight_half = weight.astype(jnp.bfloat16)
    packed = jnp.concatenate([cotangent, weight_half[None]], axis=0)
    packed_all = gathered_along(packed, "feat", 1)
    cotangent_all = packed_all[:blocks]
    weight_all = packed_all[blocks]
    nearby, cotangent_all, weight_all = lax.optimization_barrier((nearby, cotangent_all, weight_all))
    sources = jnp.einsum(
        "ts,sfk->tfk", pick_source, nearby, preferred_element_type=jnp.float32
    ).astype(jnp.bfloat16)
    forward_terms = jnp.einsum(
        "tjk,tfk->tjf", tile_values, sources, preferred_element_type=jnp.float32
    )
    aggregate = summed_by_table(add_row, forward_terms, "tb,tjf->bfj")
    aggregate = aggregate.astype(jnp.bfloat16)
    aggregate_all = gathered_along(aggregate, "feat", 1)
    column_start = lax.axis_index("feat") * width_local
    preact = jnp.einsum(
        "bij,io->boj", aggregate_all, weight_all, preferred_element_type=jnp.float32
    )
    activated = lax.dynamic_slice_in_dim(jax.nn.elu(preact), column_start, width_local, 1)
    activated = activated.astype(jnp.bfloat16)
    slope_all = (cotangent_all.astype(jnp.float32) * elu_slope(preact)).astype(jnp.bfloat16)
    node_total = cycle_size * blocks * tile_size
    grad_local = jnp.einsum("bij,boj->io", aggregate, slope_all, preferred_element_type=jnp.float32)
    grad = summed_over(grad_local, "node") * (1.0 / math.sqrt(node_total))
    back_rows = jnp.einsum(
        "io,boj->bij", weight_half, slope_all, preferred_element_type=jnp.float32
    ).astype(jnp.bfloat16)
    back_sources = jnp.einsum(
        "tb,bfj->tfj", pick_row, back_rows, preferred_element_type=jnp.float32
    ).astype(jnp.bfloat16)
    back_terms = jnp.einsum(
        "tfj,tjk->tfk", back_sources, tile_values, preferred_element_type=jnp.float32
    )
    outgoing = summed_by_table(add_source, back_terms, "ts,tfk->sfk")
    outgoing = outgoing.reshape(2 * REACH + 1, blocks, width_local, tile_size)
    feature_grad = outgoing[REACH]
    for distance in range(-REACH, REACH + 1):
        if distance != 0:
            sent = outgoing[distance + REACH].astype(jnp.bfloat16)
            feature_grad = feature_grad + passed_along(sent, "node", distance).astype(jnp.float32)
    new_first = first_decay * first_moment + (1.0 - first_decay) * grad
    new_second = second_decay * second_moment + (1.0 - second_decay) * grad * grad
    new_weight = weight - learn_rate * (new_first / first_fix) / (
        jnp.sqrt(new_second / second_fix) + adam_eps
    )
    return (activated, feature_grad, new_weight, new_first, new_second)


def solution(mesh):
    return jax.shard_map(
        per_device,
        mesh=mesh,
        in_specs=(
            P("node", "feat", None),
            P("node", None, None),
            P("node"),
            P("node"),
            P("node"),
            P("feat", None),
            P("feat", None),
            P("feat", None),
            P("node", "feat", None),
        ),
        out_specs=(
            P("node", "feat", None),
            P("node", "feat", None),
            P("feat", None),
            P("feat", None),
            P("feat", None),
        ),
        check_vma=False,
    )
```

```python
import math

import jax
import jax.numpy as jnp
from jax import lax
from jax.sharding import PartitionSpec as P

REACH = 2


first_decay = 0.9
second_decay = 0.999
learn_rate = 0.05
first_fix = 1.0 - 0.9**10
second_fix = 1.0 - 0.999**10
adam_eps = 1e-08


def passed_along(block, axis, distance):
    devices = range(lax.axis_size(axis))
    route = [((i - distance) % len(devices), i) for i in devices]
    return lax.ppermute(block, axis, route)


def gathered_along(block, axis, dim):
    size = lax.axis_size(axis)
    own = lax.axis_index(axis)
    width = block.shape[dim]
    if size & (size - 1):
        pieces = [(block, own)]
        for step in range(1, size):
            pieces.append((passed_along(block, axis, -step), (own + step) % size))
    else:
        pieces = [(block, own)]
        mask = size // 2
        while mask >= 1:
            held = jnp.stack([piece for piece, _ in pieces])
            got = lax.ppermute(held, axis, [(i, i ^ mask) for i in range(size)])
            pieces = pieces + [(got[k], index ^ mask) for k, (_, index) in enumerate(pieces)]
            mask //= 2
    shape = list(block.shape)
    shape[dim] = size * width
    whole = jnp.zeros(shape, block.dtype)
    for piece, index in pieces:
        whole = lax.dynamic_update_slice_in_dim(whole, piece, index * width, dim)
    return whole


def summed_over(block, axis):
    size = lax.axis_size(axis)
    if size & (size - 1):
        return lax.psum(block, axis)
    own = lax.axis_index(axis)
    stride = 1
    while stride < size:
        if stride * 4 <= size:
            held = [block]
            for k in (1, 2, 3):
                route = [(i, i ^ (k * stride)) for i in range(size)]
                held.append(lax.ppermute(block, axis, route))
            held = jnp.stack(held)
            member = (own // stride) % 4
            ordered = [held[m ^ member] for m in range(4)]
            block = (ordered[0] + ordered[1]) + (ordered[2] + ordered[3])
            stride *= 4
        else:
            block = block + lax.ppermute(block, axis, [(i, i ^ stride) for i in range(size)])
            stride *= 2
    return block


def summed_by_table(table, terms, spec):
    rounded = lax.reduce_precision(terms, exponent_bits=8, mantissa_bits=7)
    high = rounded.astype(jnp.bfloat16)
    low = (terms - rounded).astype(jnp.bfloat16)
    both = jnp.concatenate([high, low], axis=0)
    doubled = jnp.concatenate([table, table], axis=0).astype(jnp.bfloat16)
    return jnp.einsum(spec, doubled, both, preferred_element_type=jnp.float32)


def elu_slope(preact):
    return jnp.where(preact > 0, 1.0, jnp.exp(jnp.minimum(preact, 0.0)))


def one_hot_table(indices, count, dtype):
    return (indices[:, None] == jnp.arange(count)[None, :]).astype(dtype)


def per_device(
    features,
    tile_values,
    tile_row,
    tile_col,
    tile_count,
    weight,
    first_moment,
    second_moment,
    cotangent,
):
    cycle_size = lax.axis_size("node")
    own_node = lax.axis_index("node")
    blocks = features.shape[0]
    width_local = features.shape[1]
    tile_size = features.shape[2]
    slots = tile_values.shape[0]
    live = (jnp.arange(slots) < tile_count[0]).astype(jnp.float32)
    local_row = tile_row - own_node * blocks
    col_owner = tile_col // blocks
    col_block = tile_col % blocks
    offset = (col_owner - own_node) % cycle_size
    offset = jnp.where(offset > cycle_size // 2, offset - cycle_size, offset)
    source_slot = (offset + REACH) * blocks + col_block
    targets = (2 * REACH + 1) * blocks
    pick_source = one_hot_table(source_slot, targets, jnp.bfloat16)
    pick_row = one_hot_table(local_row, blocks, jnp.bfloat16)
    add_row = one_hot_table(local_row, blocks, jnp.float32) * live[:, None]
    add_source = one_hot_table(source_slot, targets, jnp.float32) * live[:, None]
    pieces = []
    for distance in range(-REACH, REACH + 1):
        if distance == 0:
            pieces.append(features)
        else:
            pieces.append(passed_along(features, "node", -distance))
    nearby = jnp.concatenate(pieces, axis=0)
    weight_half = weight.astype(jnp.bfloat16)
    packed = jnp.concatenate([cotangent, weight_half[None]], axis=0)
    packed_all = gathered_along(packed, "feat", 1)
    cotangent_all = packed_all[:blocks]
    weight_all = packed_all[blocks]
    nearby, cotangent_all, weight_all = lax.optimization_barrier((nearby, cotangent_all, weight_all))
    sources = jnp.einsum(
        "ts,sfk->tfk", pick_source, nearby, preferred_element_type=jnp.float32
    ).astype(jnp.bfloat16)
    tiles_turned = jnp.swapaxes(tile_values, 1, 2)
    tiles_turned, nearby = lax.optimization_barrier((tiles_turned, nearby))
    forward_terms = jnp.einsum(
        "tfk,tkj->tfj", sources, tiles_turned, preferred_element_type=jnp.float32
    )
    aggregate = summed_by_table(add_row, forward_terms, "tb,tfj->bfj")
    aggregate = aggregate.astype(jnp.bfloat16)
    aggregate_all = gathered_along(aggregate, "feat", 1)
    column_start = lax.axis_index("feat") * width_local
    preact = jnp.einsum(
        "bij,io->boj", aggregate_all, weight_all, preferred_element_type=jnp.float32
    )
    activated = lax.dynamic_slice_in_dim(jax.nn.elu(preact), column_start, width_local, 1)
    activated = activated.astype(jnp.bfloat16)
    slope_all = (cotangent_all.astype(jnp.float32) * elu_slope(preact)).astype(jnp.bfloat16)
    node_total = cycle_size * blocks * tile_size
    grad_local = jnp.einsum("bij,boj->io", aggregate, slope_all, preferred_element_type=jnp.float32)
    grad = summed_over(grad_local, "node") * (1.0 / math.sqrt(node_total))
    back_rows = jnp.einsum(
        "io,boj->bij", weight_half, slope_all, preferred_element_type=jnp.float32
    ).astype(jnp.bfloat16)
    back_sources = jnp.einsum(
        "tb,bfj->tfj", pick_row, back_rows, preferred_element_type=jnp.float32
    ).astype(jnp.bfloat16)
    back_terms = jnp.einsum(
        "tfj,tjk->tfk", back_sources, tile_values, preferred_element_type=jnp.float32
    )
    outgoing = summed_by_table(add_source, back_terms, "ts,tfk->sfk")
    outgoing = outgoing.reshape(2 * REACH + 1, blocks, width_local, tile_size)
    feature_grad = outgoing[REACH]
    for distance in range(-REACH, REACH + 1):
        if distance != 0:
            sent = outgoing[distance + REACH].astype(jnp.bfloat16)
            feature_grad = feature_grad + passed_along(sent, "node", distance).astype(jnp.float32)
    new_first = first_decay * first_moment + (1.0 - first_decay) * grad
    new_second = second_decay * second_moment + (1.0 - second_decay) * grad * grad
    new_weight = weight - learn_rate * (new_first / first_fix) / (
        jnp.sqrt(new_second / second_fix) + adam_eps
    )
    return (activated, feature_grad, new_weight, new_first, new_second)


def solution(mesh):
    return jax.shard_map(
        per_device,
        mesh=mesh,
        in_specs=(
            P("node", "feat", None),
            P("node", None, None),
            P("node"),
            P("node"),
            P("node"),
            P("feat", None),
            P("feat", None),
            P("feat", None),
            P("node", "feat", None),
        ),
        out_specs=(
            P("node", "feat", None),
            P("node", "feat", None),
            P("feat", None),
            P("feat", None),
            P("feat", None),
        ),
        check_vma=False,
    )
```

```python
import math

import jax
import jax.numpy as jnp
from jax import lax
from jax.experimental import pallas as pl
from jax.experimental.pallas import tpu as pltpu
from jax.sharding import PartitionSpec as P

REACH = 2


first_decay = 0.9
second_decay = 0.999
learn_rate = 0.05
first_fix = 1.0 - 0.9**10
second_fix = 1.0 - 0.999**10
adam_eps = 1e-08


def passed_along(block, axis, distance):
    devices = range(lax.axis_size(axis))
    route = [((i - distance) % len(devices), i) for i in devices]
    return lax.ppermute(block, axis, route)


def gathered_along(block, axis, dim):
    size = lax.axis_size(axis)
    own = lax.axis_index(axis)
    width = block.shape[dim]
    if size & (size - 1):
        pieces = [(block, own)]
        for step in range(1, size):
            pieces.append((passed_along(block, axis, -step), (own + step) % size))
    else:
        pieces = [(block, own)]
        mask = size // 2
        while mask >= 1:
            held = jnp.stack([piece for piece, _ in pieces])
            got = lax.ppermute(held, axis, [(i, i ^ mask) for i in range(size)])
            pieces = pieces + [(got[k], index ^ mask) for k, (_, index) in enumerate(pieces)]
            mask //= 2
    shape = list(block.shape)
    shape[dim] = size * width
    whole = jnp.zeros(shape, block.dtype)
    for piece, index in pieces:
        whole = lax.dynamic_update_slice_in_dim(whole, piece, index * width, dim)
    return whole


def summed_over(block, axis):
    size = lax.axis_size(axis)
    if size & (size - 1):
        return lax.psum(block, axis)
    own = lax.axis_index(axis)
    stride = 1
    while stride < size:
        if stride * 4 <= size:
            held = [block]
            for k in (1, 2, 3):
                route = [(i, i ^ (k * stride)) for i in range(size)]
                held.append(lax.ppermute(block, axis, route))
            held = jnp.stack(held)
            member = (own // stride) % 4
            ordered = [held[m ^ member] for m in range(4)]
            block = (ordered[0] + ordered[1]) + (ordered[2] + ordered[3])
            stride *= 4
        else:
            block = block + lax.ppermute(block, axis, [(i, i ^ stride) for i in range(size)])
            stride *= 2
    return block


def summed_by_table(table, terms, spec):
    rounded = lax.reduce_precision(terms, exponent_bits=8, mantissa_bits=7)
    high = rounded.astype(jnp.bfloat16)
    low = (terms - rounded).astype(jnp.bfloat16)
    both = jnp.concatenate([high, low], axis=0)
    doubled = jnp.concatenate([table, table], axis=0).astype(jnp.bfloat16)
    return jnp.einsum(spec, doubled, both, preferred_element_type=jnp.float32)


def elu_slope(preact):
    return jnp.where(preact > 0, 1.0, jnp.exp(jnp.minimum(preact, 0.0)))


def gathered_terms_kernel(source_ref, row_ref, count_ref, nearby_ref, tiles_ref, out_ref, acc_ref):
    step = pl.program_id(0)
    per_step = tiles_ref.shape[0]

    @pl.when(step == 0)
    def _():
        acc_ref[...] = jnp.zeros_like(acc_ref)

    for t in range(per_step):
        slot = step * per_step + t

        @pl.when(slot < count_ref[0])
        def _():
            picked = nearby_ref[source_ref[slot]]
            term = jnp.dot(tiles_ref[t], picked, preferred_element_type=jnp.float32)
            row = row_ref[slot]
            acc_ref[row] = acc_ref[row] + term

    @pl.when(step == pl.num_programs(0) - 1)
    def _():
        out_ref[...] = acc_ref[...]


def aggregate_by_kernel(source_slot, local_row, count, nearby_turned, tile_values, blocks):
    slots, tile, _ = tile_values.shape
    width = nearby_turned.shape[2]
    per_step = 16
    spec = pltpu.PrefetchScalarGridSpec(
        num_scalar_prefetch=3,
        grid=(slots // per_step,),
        in_specs=[
            pl.BlockSpec(nearby_turned.shape, lambda i, *_: (0, 0, 0)),
            pl.BlockSpec((per_step, tile, tile), lambda i, *_: (i, 0, 0)),
        ],
        out_specs=pl.BlockSpec((blocks, tile, width), lambda i, *_: (0, 0, 0)),
        scratch_shapes=[pltpu.VMEM((blocks, tile, width), jnp.float32)],
    )
    return pl.pallas_call(
        gathered_terms_kernel,
        grid_spec=spec,
        out_shape=jax.ShapeDtypeStruct((blocks, tile, width), jnp.float32),
        compiler_params=pltpu.CompilerParams(dimension_semantics=("arbitrary",)),
    )(source_slot, local_row, count, nearby_turned, tile_values)


def one_hot_table(indices, count, dtype):
    return (indices[:, None] == jnp.arange(count)[None, :]).astype(dtype)


def per_device(
    features,
    tile_values,
    tile_row,
    tile_col,
    tile_count,
    weight,
    first_moment,
    second_moment,
    cotangent,
):
    cycle_size = lax.axis_size("node")
    own_node = lax.axis_index("node")
    blocks = features.shape[0]
    width_local = features.shape[1]
    tile_size = features.shape[2]
    slots = tile_values.shape[0]
    live = (jnp.arange(slots) < tile_count[0]).astype(jnp.float32)
    local_row = tile_row - own_node * blocks
    col_owner = tile_col // blocks
    col_block = tile_col % blocks
    offset = (col_owner - own_node) % cycle_size
    offset = jnp.where(offset > cycle_size // 2, offset - cycle_size, offset)
    source_slot = (offset + REACH) * blocks + col_block
    targets = (2 * REACH + 1) * blocks
    source_slot = jnp.clip(source_slot, 0, targets - 1)
    local_row = jnp.clip(local_row, 0, blocks - 1)
    pick_row = one_hot_table(local_row, blocks, jnp.bfloat16)
    add_source = one_hot_table(source_slot, targets, jnp.float32) * live[:, None]
    pieces = []
    for distance in range(-REACH, REACH + 1):
        if distance == 0:
            pieces.append(features)
        else:
            pieces.append(passed_along(features, "node", -distance))
    nearby = jnp.concatenate(pieces, axis=0)
    weight_half = weight.astype(jnp.bfloat16)
    packed = jnp.concatenate([cotangent, weight_half[None]], axis=0)
    packed_all = gathered_along(packed, "feat", 1)
    cotangent_all = packed_all[:blocks]
    weight_all = packed_all[blocks]
    nearby, cotangent_all, weight_all = lax.optimization_barrier((nearby, cotangent_all, weight_all))
    turned = aggregate_by_kernel(
        source_slot, local_row, tile_count, jnp.swapaxes(nearby, 1, 2), tile_values, blocks
    )
    aggregate = jnp.swapaxes(turned, 1, 2)
    aggregate = aggregate.astype(jnp.bfloat16)
    aggregate_all = gathered_along(aggregate, "feat", 1)
    column_start = lax.axis_index("feat") * width_local
    preact = jnp.einsum(
        "bij,io->boj", aggregate_all, weight_all, preferred_element_type=jnp.float32
    )
    activated = lax.dynamic_slice_in_dim(jax.nn.elu(preact), column_start, width_local, 1)
    activated = activated.astype(jnp.bfloat16)
    slope_all = (cotangent_all.astype(jnp.float32) * elu_slope(preact)).astype(jnp.bfloat16)
    node_total = cycle_size * blocks * tile_size
    grad_local = jnp.einsum("bij,boj->io", aggregate, slope_all, preferred_element_type=jnp.float32)
    grad = summed_over(grad_local, "node") * (1.0 / math.sqrt(node_total))
    back_rows = jnp.einsum(
        "io,boj->bij", weight_half, slope_all, preferred_element_type=jnp.float32
    ).astype(jnp.bfloat16)
    back_sources = jnp.einsum(
        "tb,bfj->tfj", pick_row, back_rows, preferred_element_type=jnp.float32
    ).astype(jnp.bfloat16)
    back_terms = jnp.einsum(
        "tfj,tjk->tfk", back_sources, tile_values, preferred_element_type=jnp.float32
    )
    outgoing = summed_by_table(add_source, back_terms, "ts,tfk->sfk")
    outgoing = outgoing.reshape(2 * REACH + 1, blocks, width_local, tile_size)
    feature_grad = outgoing[REACH]
    for distance in range(-REACH, REACH + 1):
        if distance != 0:
            sent = outgoing[distance + REACH].astype(jnp.bfloat16)
            feature_grad = feature_grad + passed_along(sent, "node", distance).astype(jnp.float32)
    new_first = first_decay * first_moment + (1.0 - first_decay) * grad
    new_second = second_decay * second_moment + (1.0 - second_decay) * grad * grad
    new_weight = weight - learn_rate * (new_first / first_fix) / (
        jnp.sqrt(new_second / second_fix) + adam_eps
    )
    return (activated, feature_grad, new_weight, new_first, new_second)


def solution(mesh):
    return jax.shard_map(
        per_device,
        mesh=mesh,
        in_specs=(
            P("node", "feat", None),
            P("node", None, None),
            P("node"),
            P("node"),
            P("node"),
            P("feat", None),
            P("feat", None),
            P("feat", None),
            P("node", "feat", None),
        ),
        out_specs=(
            P("node", "feat", None),
            P("node", "feat", None),
            P("feat", None),
            P("feat", None),
            P("feat", None),
        ),
        check_vma=False,
    )
```

```python
import math

import jax
import jax.numpy as jnp
from jax import lax
from jax.experimental import pallas as pl
from jax.experimental.pallas import tpu as pltpu
from jax.sharding import PartitionSpec as P

REACH = 2


first_decay = 0.9
second_decay = 0.999
learn_rate = 0.05
first_fix = 1.0 - 0.9**10
second_fix = 1.0 - 0.999**10
adam_eps = 1e-08


def passed_along(block, axis, distance):
    devices = range(lax.axis_size(axis))
    route = [((i - distance) % len(devices), i) for i in devices]
    return lax.ppermute(block, axis, route)


def gathered_along(block, axis, dim):
    size = lax.axis_size(axis)
    own = lax.axis_index(axis)
    width = block.shape[dim]
    if size & (size - 1):
        pieces = [(block, own)]
        for step in range(1, size):
            pieces.append((passed_along(block, axis, -step), (own + step) % size))
    else:
        pieces = [(block, own)]
        mask = size // 2
        while mask >= 1:
            held = jnp.stack([piece for piece, _ in pieces])
            got = lax.ppermute(held, axis, [(i, i ^ mask) for i in range(size)])
            pieces = pieces + [(got[k], index ^ mask) for k, (_, index) in enumerate(pieces)]
            mask //= 2
    shape = list(block.shape)
    shape[dim] = size * width
    whole = jnp.zeros(shape, block.dtype)
    for piece, index in pieces:
        whole = lax.dynamic_update_slice_in_dim(whole, piece, index * width, dim)
    return whole


def summed_over(block, axis):
    size = lax.axis_size(axis)
    if size & (size - 1):
        return lax.psum(block, axis)
    own = lax.axis_index(axis)
    stride = 1
    while stride < size:
        if stride * 4 <= size:
            held = [block]
            for k in (1, 2, 3):
                route = [(i, i ^ (k * stride)) for i in range(size)]
                held.append(lax.ppermute(block, axis, route))
            held = jnp.stack(held)
            member = (own // stride) % 4
            ordered = [held[m ^ member] for m in range(4)]
            block = (ordered[0] + ordered[1]) + (ordered[2] + ordered[3])
            stride *= 4
        else:
            block = block + lax.ppermute(block, axis, [(i, i ^ stride) for i in range(size)])
            stride *= 2
    return block


def summed_by_table(table, terms, spec):
    rounded = lax.reduce_precision(terms, exponent_bits=8, mantissa_bits=7)
    high = rounded.astype(jnp.bfloat16)
    low = (terms - rounded).astype(jnp.bfloat16)
    both = jnp.concatenate([high, low], axis=0)
    doubled = jnp.concatenate([table, table], axis=0).astype(jnp.bfloat16)
    return jnp.einsum(spec, doubled, both, preferred_element_type=jnp.float32)


def elu_slope(preact):
    return jnp.where(preact > 0, 1.0, jnp.exp(jnp.minimum(preact, 0.0)))


def gathered_terms_kernel(source_ref, row_ref, count_ref, nearby_ref, tiles_ref, out_ref, acc_ref):
    step = pl.program_id(0)
    per_step = tiles_ref.shape[0]

    @pl.when(step == 0)
    def _():
        acc_ref[...] = jnp.zeros_like(acc_ref)

    terms = []
    for t in range(per_step):
        slot = step * per_step + t
        picked = nearby_ref[source_ref[slot]]
        term = lax.dot_general(
            tiles_ref[t], picked, (((1,), (1,)), ((), ())), preferred_element_type=jnp.float32
        )
        terms.append(jnp.where(slot < count_ref[0], term, 0.0))
    for t in range(per_step):
        row = row_ref[step * per_step + t]
        acc_ref[row] = acc_ref[row] + terms[t]

    @pl.when(step == pl.num_programs(0) - 1)
    def _():
        out_ref[...] = acc_ref[...]


def aggregate_by_kernel(source_slot, local_row, count, nearby, tile_values, blocks):
    slots, tile, _ = tile_values.shape
    width = nearby.shape[1]
    per_step = 16
    spec = pltpu.PrefetchScalarGridSpec(
        num_scalar_prefetch=3,
        grid=(slots // per_step,),
        in_specs=[
            pl.BlockSpec(nearby.shape, lambda i, *_: (0, 0, 0)),
            pl.BlockSpec((per_step, tile, tile), lambda i, *_: (i, 0, 0)),
        ],
        out_specs=pl.BlockSpec((blocks, tile, width), lambda i, *_: (0, 0, 0)),
        scratch_shapes=[pltpu.VMEM((blocks, tile, width), jnp.float32)],
    )
    return pl.pallas_call(
        gathered_terms_kernel,
        grid_spec=spec,
        out_shape=jax.ShapeDtypeStruct((blocks, tile, width), jnp.float32),
        compiler_params=pltpu.CompilerParams(dimension_semantics=("arbitrary",)),
    )(source_slot, local_row, count, nearby, tile_values)


def one_hot_table(indices, count, dtype):
    return (indices[:, None] == jnp.arange(count)[None, :]).astype(dtype)


def per_device(
    features,
    tile_values,
    tile_row,
    tile_col,
    tile_count,
    weight,
    first_moment,
    second_moment,
    cotangent,
):
    cycle_size = lax.axis_size("node")
    own_node = lax.axis_index("node")
    blocks = features.shape[0]
    width_local = features.shape[1]
    tile_size = features.shape[2]
    slots = tile_values.shape[0]
    live = (jnp.arange(slots) < tile_count[0]).astype(jnp.float32)
    local_row = tile_row - own_node * blocks
    col_owner = tile_col // blocks
    col_block = tile_col % blocks
    offset = (col_owner - own_node) % cycle_size
    offset = jnp.where(offset > cycle_size // 2, offset - cycle_size, offset)
    source_slot = (offset + REACH) * blocks + col_block
    targets = (2 * REACH + 1) * blocks
    source_slot = jnp.clip(source_slot, 0, targets - 1)
    local_row = jnp.clip(local_row, 0, blocks - 1)
    pick_row = one_hot_table(local_row, blocks, jnp.bfloat16)
    add_source = one_hot_table(source_slot, targets, jnp.float32) * live[:, None]
    pieces = []
    for distance in range(-REACH, REACH + 1):
        if distance == 0:
            pieces.append(features)
        else:
            pieces.append(passed_along(features, "node", -distance))
    nearby = jnp.concatenate(pieces, axis=0)
    weight_half = weight.astype(jnp.bfloat16)
    packed = jnp.concatenate([cotangent, weight_half[None]], axis=0)
    packed_all = gathered_along(packed, "feat", 1)
    cotangent_all = packed_all[:blocks]
    weight_all = packed_all[blocks]
    nearby, cotangent_all, weight_all = lax.optimization_barrier((nearby, cotangent_all, weight_all))
    turned = aggregate_by_kernel(
        source_slot, local_row, tile_count, nearby, tile_values, blocks
    )
    aggregate = jnp.swapaxes(turned, 1, 2)
    aggregate = aggregate.astype(jnp.bfloat16)
    aggregate_all = gathered_along(aggregate, "feat", 1)
    column_start = lax.axis_index("feat") * width_local
    preact = jnp.einsum(
        "bij,io->boj", aggregate_all, weight_all, preferred_element_type=jnp.float32
    )
    activated = lax.dynamic_slice_in_dim(jax.nn.elu(preact), column_start, width_local, 1)
    activated = activated.astype(jnp.bfloat16)
    slope_all = (cotangent_all.astype(jnp.float32) * elu_slope(preact)).astype(jnp.bfloat16)
    node_total = cycle_size * blocks * tile_size
    grad_local = jnp.einsum("bij,boj->io", aggregate, slope_all, preferred_element_type=jnp.float32)
    grad = summed_over(grad_local, "node") * (1.0 / math.sqrt(node_total))
    back_rows = jnp.einsum(
        "io,boj->bij", weight_half, slope_all, preferred_element_type=jnp.float32
    ).astype(jnp.bfloat16)
    back_sources = jnp.einsum(
        "tb,bfj->tfj", pick_row, back_rows, preferred_element_type=jnp.float32
    ).astype(jnp.bfloat16)
    back_terms = jnp.einsum(
        "tfj,tjk->tfk", back_sources, tile_values, preferred_element_type=jnp.float32
    )
    outgoing = summed_by_table(add_source, back_terms, "ts,tfk->sfk")
    outgoing = outgoing.reshape(2 * REACH + 1, blocks, width_local, tile_size)
    feature_grad = outgoing[REACH]
    for distance in range(-REACH, REACH + 1):
        if distance != 0:
            sent = outgoing[distance + REACH].astype(jnp.bfloat16)
            feature_grad = feature_grad + passed_along(sent, "node", distance).astype(jnp.float32)
    new_first = first_decay * first_moment + (1.0 - first_decay) * grad
    new_second = second_decay * second_moment + (1.0 - second_decay) * grad * grad
    new_weight = weight - learn_rate * (new_first / first_fix) / (
        jnp.sqrt(new_second / second_fix) + adam_eps
    )
    return (activated, feature_grad, new_weight, new_first, new_second)


def solution(mesh):
    return jax.shard_map(
        per_device,
        mesh=mesh,
        in_specs=(
            P("node", "feat", None),
            P("node", None, None),
            P("node"),
            P("node"),
            P("node"),
            P("feat", None),
            P("feat", None),
            P("feat", None),
            P("node", "feat", None),
        ),
        out_specs=(
            P("node", "feat", None),
            P("node", "feat", None),
            P("feat", None),
            P("feat", None),
            P("feat", None),
        ),
        check_vma=False,
    )
```

```python
import math

import jax
import jax.numpy as jnp
from jax import lax
from jax.experimental import pallas as pl
from jax.experimental.pallas import tpu as pltpu
from jax.sharding import PartitionSpec as P

REACH = 2


first_decay = 0.9
second_decay = 0.999
learn_rate = 0.05
first_fix = 1.0 - 0.9**10
second_fix = 1.0 - 0.999**10
adam_eps = 1e-08


def passed_along(block, axis, distance):
    devices = range(lax.axis_size(axis))
    route = [((i - distance) % len(devices), i) for i in devices]
    return lax.ppermute(block, axis, route)


def gathered_along(block, axis, dim):
    size = lax.axis_size(axis)
    own = lax.axis_index(axis)
    width = block.shape[dim]
    if size & (size - 1):
        pieces = [(block, own)]
        for step in range(1, size):
            pieces.append((passed_along(block, axis, -step), (own + step) % size))
    else:
        pieces = [(block, own)]
        mask = size // 2
        while mask >= 1:
            held = jnp.stack([piece for piece, _ in pieces])
            got = lax.ppermute(held, axis, [(i, i ^ mask) for i in range(size)])
            pieces = pieces + [(got[k], index ^ mask) for k, (_, index) in enumerate(pieces)]
            mask //= 2
    shape = list(block.shape)
    shape[dim] = size * width
    whole = jnp.zeros(shape, block.dtype)
    for piece, index in pieces:
        whole = lax.dynamic_update_slice_in_dim(whole, piece, index * width, dim)
    return whole


def summed_over(block, axis):
    size = lax.axis_size(axis)
    if size & (size - 1):
        return lax.psum(block, axis)
    own = lax.axis_index(axis)
    stride = 1
    while stride < size:
        if stride * 4 <= size:
            held = [block]
            for k in (1, 2, 3):
                route = [(i, i ^ (k * stride)) for i in range(size)]
                held.append(lax.ppermute(block, axis, route))
            held = jnp.stack(held)
            member = (own // stride) % 4
            ordered = [held[m ^ member] for m in range(4)]
            block = (ordered[0] + ordered[1]) + (ordered[2] + ordered[3])
            stride *= 4
        else:
            block = block + lax.ppermute(block, axis, [(i, i ^ stride) for i in range(size)])
            stride *= 2
    return block


def summed_by_table(table, terms, spec):
    rounded = lax.reduce_precision(terms, exponent_bits=8, mantissa_bits=7)
    high = rounded.astype(jnp.bfloat16)
    low = (terms - rounded).astype(jnp.bfloat16)
    both = jnp.concatenate([high, low], axis=0)
    doubled = jnp.concatenate([table, table], axis=0).astype(jnp.bfloat16)
    return jnp.einsum(spec, doubled, both, preferred_element_type=jnp.float32)


def elu_slope(preact):
    return jnp.where(preact > 0, 1.0, jnp.exp(jnp.minimum(preact, 0.0)))


def gathered_terms_kernel(source_ref, row_ref, count_ref, nearby_ref, tiles_ref, out_ref, acc_ref):
    step = pl.program_id(0)
    per_step = tiles_ref.shape[0]

    @pl.when(step == 0)
    def _():
        acc_ref[...] = jnp.zeros_like(acc_ref)

    terms = []
    for t in range(per_step):
        slot = step * per_step + t
        picked = nearby_ref[source_ref[slot]]
        term = lax.dot_general(
            picked, tiles_ref[t], (((1,), (1,)), ((), ())), preferred_element_type=jnp.float32
        )
        terms.append(jnp.where(slot < count_ref[0], term, 0.0))
    for t in range(per_step):
        row = row_ref[step * per_step + t]
        acc_ref[row] = acc_ref[row] + terms[t]

    @pl.when(step == pl.num_programs(0) - 1)
    def _():
        out_ref[...] = acc_ref[...]


def aggregate_by_kernel(source_slot, local_row, count, nearby, tile_values, blocks):
    slots, tile, _ = tile_values.shape
    width = nearby.shape[1]
    per_step = 16
    spec = pltpu.PrefetchScalarGridSpec(
        num_scalar_prefetch=3,
        grid=(slots // per_step,),
        in_specs=[
            pl.BlockSpec(nearby.shape, lambda i, *_: (0, 0, 0)),
            pl.BlockSpec((per_step, tile, tile), lambda i, *_: (i, 0, 0)),
        ],
        out_specs=pl.BlockSpec((blocks, width, tile), lambda i, *_: (0, 0, 0)),
        scratch_shapes=[pltpu.VMEM((blocks, width, tile), jnp.float32)],
    )
    return pl.pallas_call(
        gathered_terms_kernel,
        grid_spec=spec,
        out_shape=jax.ShapeDtypeStruct((blocks, width, tile), jnp.float32),
        compiler_params=pltpu.CompilerParams(dimension_semantics=("arbitrary",)),
    )(source_slot, local_row, count, nearby, tile_values)


def one_hot_table(indices, count, dtype):
    return (indices[:, None] == jnp.arange(count)[None, :]).astype(dtype)


def per_device(
    features,
    tile_values,
    tile_row,
    tile_col,
    tile_count,
    weight,
    first_moment,
    second_moment,
    cotangent,
):
    cycle_size = lax.axis_size("node")
    own_node = lax.axis_index("node")
    blocks = features.shape[0]
    width_local = features.shape[1]
    tile_size = features.shape[2]
    slots = tile_values.shape[0]
    live = (jnp.arange(slots) < tile_count[0]).astype(jnp.float32)
    local_row = tile_row - own_node * blocks
    col_owner = tile_col // blocks
    col_block = tile_col % blocks
    offset = (col_owner - own_node) % cycle_size
    offset = jnp.where(offset > cycle_size // 2, offset - cycle_size, offset)
    source_slot = (offset + REACH) * blocks + col_block
    targets = (2 * REACH + 1) * blocks
    source_slot = jnp.clip(source_slot, 0, targets - 1)
    local_row = jnp.clip(local_row, 0, blocks - 1)
    pick_row = one_hot_table(local_row, blocks, jnp.bfloat16)
    add_source = one_hot_table(source_slot, targets, jnp.float32) * live[:, None]
    pieces = []
    for distance in range(-REACH, REACH + 1):
        if distance == 0:
            pieces.append(features)
        else:
            pieces.append(passed_along(features, "node", -distance))
    nearby = jnp.concatenate(pieces, axis=0)
    weight_half = weight.astype(jnp.bfloat16)
    packed = jnp.concatenate([cotangent, weight_half[None]], axis=0)
    packed_all = gathered_along(packed, "feat", 1)
    cotangent_all = packed_all[:blocks]
    weight_all = packed_all[blocks]
    nearby, cotangent_all, weight_all = lax.optimization_barrier((nearby, cotangent_all, weight_all))
    turned = aggregate_by_kernel(
        source_slot, local_row, tile_count, nearby, tile_values, blocks
    )
    aggregate = turned
    aggregate = aggregate.astype(jnp.bfloat16)
    aggregate_all = gathered_along(aggregate, "feat", 1)
    column_start = lax.axis_index("feat") * width_local
    preact = jnp.einsum(
        "bij,io->boj", aggregate_all, weight_all, preferred_element_type=jnp.float32
    )
    activated = lax.dynamic_slice_in_dim(jax.nn.elu(preact), column_start, width_local, 1)
    activated = activated.astype(jnp.bfloat16)
    slope_all = (cotangent_all.astype(jnp.float32) * elu_slope(preact)).astype(jnp.bfloat16)
    node_total = cycle_size * blocks * tile_size
    grad_local = jnp.einsum("bij,boj->io", aggregate, slope_all, preferred_element_type=jnp.float32)
    grad = summed_over(grad_local, "node") * (1.0 / math.sqrt(node_total))
    back_rows = jnp.einsum(
        "io,boj->bij", weight_half, slope_all, preferred_element_type=jnp.float32
    ).astype(jnp.bfloat16)
    back_sources = jnp.einsum(
        "tb,bfj->tfj", pick_row, back_rows, preferred_element_type=jnp.float32
    ).astype(jnp.bfloat16)
    back_terms = jnp.einsum(
        "tfj,tjk->tfk", back_sources, tile_values, preferred_element_type=jnp.float32
    )
    outgoing = summed_by_table(add_source, back_terms, "ts,tfk->sfk")
    outgoing = outgoing.reshape(2 * REACH + 1, blocks, width_local, tile_size)
    feature_grad = outgoing[REACH]
    for distance in range(-REACH, REACH + 1):
        if distance != 0:
            sent = outgoing[distance + REACH].astype(jnp.bfloat16)
            feature_grad = feature_grad + passed_along(sent, "node", distance).astype(jnp.float32)
    new_first = first_decay * first_moment + (1.0 - first_decay) * grad
    new_second = second_decay * second_moment + (1.0 - second_decay) * grad * grad
    new_weight = weight - learn_rate * (new_first / first_fix) / (
        jnp.sqrt(new_second / second_fix) + adam_eps
    )
    return (activated, feature_grad, new_weight, new_first, new_second)


def solution(mesh):
    return jax.shard_map(
        per_device,
        mesh=mesh,
        in_specs=(
            P("node", "feat", None),
            P("node", None, None),
            P("node"),
            P("node"),
            P("node"),
            P("feat", None),
            P("feat", None),
            P("feat", None),
            P("node", "feat", None),
        ),
        out_specs=(
            P("node", "feat", None),
            P("node", "feat", None),
            P("feat", None),
            P("feat", None),
            P("feat", None),
        ),
        check_vma=False,
    )
```

```python
import math

import jax
import jax.numpy as jnp
from jax import lax
from jax.sharding import PartitionSpec as P

REACH = 2


first_decay = 0.9
second_decay = 0.999
learn_rate = 0.05
first_fix = 1.0 - 0.9**10
second_fix = 1.0 - 0.999**10
adam_eps = 1e-08


def passed_along(block, axis, distance):
    devices = range(lax.axis_size(axis))
    route = [((i - distance) % len(devices), i) for i in devices]
    return lax.ppermute(block, axis, route)


def gathered_along(block, axis, dim):
    size = lax.axis_size(axis)
    own = lax.axis_index(axis)
    width = block.shape[dim]
    if size & (size - 1):
        pieces = [(block, own)]
        for step in range(1, size):
            pieces.append((passed_along(block, axis, -step), (own + step) % size))
    else:
        pieces = [(block, own)]
        mask = size // 2
        while mask >= 1:
            held = jnp.stack([piece for piece, _ in pieces])
            got = lax.ppermute(held, axis, [(i, i ^ mask) for i in range(size)])
            pieces = pieces + [(got[k], index ^ mask) for k, (_, index) in enumerate(pieces)]
            mask //= 2
    shape = list(block.shape)
    shape[dim] = size * width
    whole = jnp.zeros(shape, block.dtype)
    for piece, index in pieces:
        whole = lax.dynamic_update_slice_in_dim(whole, piece, index * width, dim)
    return whole


def summed_over(block, axis):
    size = lax.axis_size(axis)
    if size & (size - 1):
        return lax.psum(block, axis)
    own = lax.axis_index(axis)
    stride = 1
    while stride < size:
        if stride * 4 <= size:
            held = [block]
            for k in (1, 2, 3):
                route = [(i, i ^ (k * stride)) for i in range(size)]
                held.append(lax.ppermute(block, axis, route))
            held = jnp.stack(held)
            member = (own // stride) % 4
            ordered = [held[m ^ member] for m in range(4)]
            block = (ordered[0] + ordered[1]) + (ordered[2] + ordered[3])
            stride *= 4
        else:
            block = block + lax.ppermute(block, axis, [(i, i ^ stride) for i in range(size)])
            stride *= 2
    return block


def summed_by_table(table, terms, spec):
    rounded = lax.reduce_precision(terms, exponent_bits=8, mantissa_bits=7)
    high = rounded.astype(jnp.bfloat16)
    low = (terms - rounded).astype(jnp.bfloat16)
    both = jnp.concatenate([high, low], axis=0)
    doubled = jnp.concatenate([table, table], axis=0).astype(jnp.bfloat16)
    return jnp.einsum(spec, doubled, both, preferred_element_type=jnp.float32)


def elu_slope(preact):
    return jnp.where(preact > 0, 1.0, jnp.exp(jnp.minimum(preact, 0.0)))


def one_hot_table(indices, count, dtype):
    return (indices[:, None] == jnp.arange(count)[None, :]).astype(dtype)


def per_device(
    features,
    tile_values,
    tile_row,
    tile_col,
    tile_count,
    weight,
    first_moment,
    second_moment,
    cotangent,
):
    cycle_size = lax.axis_size("node")
    own_node = lax.axis_index("node")
    blocks = features.shape[0]
    width_local = features.shape[1]
    tile_size = features.shape[2]
    slots = tile_values.shape[0]
    live = (jnp.arange(slots) < tile_count[0]).astype(jnp.float32)
    local_row = tile_row - own_node * blocks
    col_owner = tile_col // blocks
    col_block = tile_col % blocks
    offset = (col_owner - own_node) % cycle_size
    offset = jnp.where(offset > cycle_size // 2, offset - cycle_size, offset)
    source_slot = (offset + REACH) * blocks + col_block
    targets = (2 * REACH + 1) * blocks
    add_row = one_hot_table(local_row, blocks, jnp.float32) * live[:, None]
    add_source = one_hot_table(source_slot, targets, jnp.float32) * live[:, None]
    pieces = []
    for distance in range(-REACH, REACH + 1):
        if distance == 0:
            pieces.append(features)
        else:
            pieces.append(passed_along(features, "node", -distance))
    nearby = jnp.concatenate(pieces, axis=0)
    weight_half = weight.astype(jnp.bfloat16)
    packed = jnp.concatenate([cotangent, weight_half[None]], axis=0)
    packed_all = gathered_along(packed, "feat", 1)
    cotangent_all = packed_all[:blocks]
    weight_all = packed_all[blocks]
    nearby, cotangent_all, weight_all = lax.optimization_barrier((nearby, cotangent_all, weight_all))
    sources = jnp.take(nearby, jnp.clip(source_slot, 0, targets - 1), axis=0)
    forward_terms = jnp.einsum(
        "tjk,tfk->tjf", tile_values, sources, preferred_element_type=jnp.float32
    )
    aggregate = summed_by_table(add_row, forward_terms, "tb,tjf->bfj")
    aggregate = aggregate.astype(jnp.bfloat16)
    aggregate_all = gathered_along(aggregate, "feat", 1)
    column_start = lax.axis_index("feat") * width_local
    preact = jnp.einsum(
        "bij,io->boj", aggregate_all, weight_all, preferred_element_type=jnp.float32
    )
    activated = lax.dynamic_slice_in_dim(jax.nn.elu(preact), column_start, width_local, 1)
    activated = activated.astype(jnp.bfloat16)
    slope_all = (cotangent_all.astype(jnp.float32) * elu_slope(preact)).astype(jnp.bfloat16)
    node_total = cycle_size * blocks * tile_size
    grad_local = jnp.einsum("bij,boj->io", aggregate, slope_all, preferred_element_type=jnp.float32)
    grad = summed_over(grad_local, "node") * (1.0 / math.sqrt(node_total))
    back_rows = jnp.einsum(
        "io,boj->bij", weight_half, slope_all, preferred_element_type=jnp.float32
    ).astype(jnp.bfloat16)
    back_sources = jnp.take(back_rows, jnp.clip(local_row, 0, blocks - 1), axis=0)
    back_terms = jnp.einsum(
        "tfj,tjk->tfk", back_sources, tile_values, preferred_element_type=jnp.float32
    )
    outgoing = summed_by_table(add_source, back_terms, "ts,tfk->sfk")
    outgoing = outgoing.reshape(2 * REACH + 1, blocks, width_local, tile_size)
    feature_grad = outgoing[REACH]
    for distance in range(-REACH, REACH + 1):
        if distance != 0:
            sent = outgoing[distance + REACH].astype(jnp.bfloat16)
            feature_grad = feature_grad + passed_along(sent, "node", distance).astype(jnp.float32)
    new_first = first_decay * first_moment + (1.0 - first_decay) * grad
    new_second = second_decay * second_moment + (1.0 - second_decay) * grad * grad
    new_weight = weight - learn_rate * (new_first / first_fix) / (
        jnp.sqrt(new_second / second_fix) + adam_eps
    )
    return (activated, feature_grad, new_weight, new_first, new_second)


def solution(mesh):
    return jax.shard_map(
        per_device,
        mesh=mesh,
        in_specs=(
            P("node", "feat", None),
            P("node", None, None),
            P("node"),
            P("node"),
            P("node"),
            P("feat", None),
            P("feat", None),
            P("feat", None),
            P("node", "feat", None),
        ),
        out_specs=(
            P("node", "feat", None),
            P("node", "feat", None),
            P("feat", None),
            P("feat", None),
            P("feat", None),
        ),
        check_vma=False,
    )
```

```python
import math

import jax
import jax.numpy as jnp
from jax import lax
from jax.sharding import PartitionSpec as P

REACH = 2


first_decay = 0.9
second_decay = 0.999
learn_rate = 0.05
first_fix = 1.0 - 0.9**10
second_fix = 1.0 - 0.999**10
adam_eps = 1e-08


def passed_along(block, axis, distance):
    devices = range(lax.axis_size(axis))
    route = [((i - distance) % len(devices), i) for i in devices]
    return lax.ppermute(block, axis, route)


def gathered_along(block, axis, dim, beside=None):
    size = lax.axis_size(axis)
    own = lax.axis_index(axis)
    width = block.shape[dim]
    if size & (size - 1):
        pieces = [(block, own)]
        for step in range(1, size):
            pieces.append((passed_along(block, axis, -step), (own + step) % size))
        if beside is not None:
            arrays, beside = lax.optimization_barrier(([piece for piece, _ in pieces], beside))
            pieces = [(array, index) for array, (_, index) in zip(arrays, pieces)]
    else:
        pieces = [(block, own)]
        mask = size // 2
        while mask >= 1:
            held = jnp.stack([piece for piece, _ in pieces])
            got = lax.ppermute(held, axis, [(i, i ^ mask) for i in range(size)])
            if beside is not None and mask == size // 2:
                got, beside = lax.optimization_barrier((got, beside))
            pieces = pieces + [(got[k], index ^ mask) for k, (_, index) in enumerate(pieces)]
            mask //= 2
    shape = list(block.shape)
    shape[dim] = size * width
    whole = jnp.zeros(shape, block.dtype)
    for piece, index in pieces:
        whole = lax.dynamic_update_slice_in_dim(whole, piece, index * width, dim)
    if beside is None:
        return whole
    return whole, beside


def summed_over(block, axis):
    size = lax.axis_size(axis)
    if size & (size - 1):
        return lax.psum(block, axis)
    mask = 1
    while mask < size:
        block = block + lax.ppermute(block, axis, [(i, i ^ mask) for i in range(size)])
        mask *= 2
    return block


def summed_by_table(table, terms, spec):
    rounded = lax.reduce_precision(terms, exponent_bits=8, mantissa_bits=7)
    high = rounded.astype(jnp.bfloat16)
    low = (terms - rounded).astype(jnp.bfloat16)
    both = jnp.concatenate([high, low], axis=0)
    doubled = jnp.concatenate([table, table], axis=0).astype(jnp.bfloat16)
    return jnp.einsum(spec, doubled, both, preferred_element_type=jnp.float32)


def elu_slope(preact):
    return jnp.where(preact > 0, 1.0, jnp.exp(jnp.minimum(preact, 0.0)))


def one_hot_table(indices, count, dtype):
    return (indices[:, None] == jnp.arange(count)[None, :]).astype(dtype)


def per_device(
    features,
    tile_values,
    tile_row,
    tile_col,
    tile_count,
    weight,
    first_moment,
    second_moment,
    cotangent,
):
    cycle_size = lax.axis_size("node")
    own_node = lax.axis_index("node")
    blocks = features.shape[0]
    width_local = features.shape[1]
    tile_size = features.shape[2]
    slots = tile_values.shape[0]
    live = (jnp.arange(slots) < tile_count[0]).astype(jnp.float32)
    local_row = tile_row - own_node * blocks
    col_owner = tile_col // blocks
    col_block = tile_col % blocks
    offset = (col_owner - own_node) % cycle_size
    offset = jnp.where(offset > cycle_size // 2, offset - cycle_size, offset)
    source_slot = (offset + REACH) * blocks + col_block
    targets = (2 * REACH + 1) * blocks
    pick_source = one_hot_table(source_slot, targets, jnp.bfloat16)
    pick_row = one_hot_table(local_row, blocks, jnp.bfloat16)
    add_row = one_hot_table(local_row, blocks, jnp.float32) * live[:, None]
    add_source = one_hot_table(source_slot, targets, jnp.float32) * live[:, None]
    pieces = []
    for distance in range(-REACH, REACH + 1):
        if distance == 0:
            pieces.append(features)
        else:
            pieces.append(passed_along(features, "node", -distance))
    nearby = jnp.concatenate(pieces, axis=0)
    weight_half = weight.astype(jnp.bfloat16)
    packed = jnp.concatenate([cotangent, weight_half[None]], axis=0)
    packed_all, nearby = gathered_along(packed, "feat", 1, beside=nearby)
    cotangent_all = packed_all[:blocks]
    weight_all = packed_all[blocks]
    sources = jnp.einsum(
        "ts,sfk->tfk", pick_source, nearby, preferred_element_type=jnp.float32
    ).astype(jnp.bfloat16)
    forward_terms = jnp.einsum(
        "tfk,tjk->tfj", sources, tile_values, preferred_element_type=jnp.float32
    )
    aggregate = summed_by_table(add_row, forward_terms, "tb,tfj->bfj")
    aggregate = aggregate.astype(jnp.bfloat16)
    aggregate_all = gathered_along(aggregate, "feat", 1)
    column_start = lax.axis_index("feat") * width_local
    preact = jnp.einsum(
        "bij,io->boj", aggregate_all, weight_all, preferred_element_type=jnp.float32
    )
    activated = lax.dynamic_slice_in_dim(jax.nn.elu(preact), column_start, width_local, 1)
    activated = activated.astype(jnp.bfloat16)
    slope_all = (cotangent_all.astype(jnp.float32) * elu_slope(preact)).astype(jnp.bfloat16)
    node_total = cycle_size * blocks * tile_size
    grad_local = jnp.einsum("bij,boj->io", aggregate, slope_all, preferred_element_type=jnp.float32)
    grad = summed_over(grad_local, "node") * (1.0 / math.sqrt(node_total))
    back_rows = jnp.einsum(
        "io,boj->bij", weight_half, slope_all, preferred_element_type=jnp.float32
    ).astype(jnp.bfloat16)
    back_sources = jnp.einsum(
        "tb,bfj->tfj", pick_row, back_rows, preferred_element_type=jnp.float32
    ).astype(jnp.bfloat16)
    back_terms = jnp.einsum(
        "tfj,tjk->tfk", back_sources, tile_values, preferred_element_type=jnp.float32
    )
    outgoing = summed_by_table(add_source, back_terms, "ts,tfk->sfk")
    outgoing = outgoing.reshape(2 * REACH + 1, blocks, width_local, tile_size)
    feature_grad = outgoing[REACH]
    for distance in range(-REACH, REACH + 1):
        if distance != 0:
            sent = outgoing[distance + REACH].astype(jnp.bfloat16)
            feature_grad = feature_grad + passed_along(sent, "node", distance).astype(jnp.float32)
    new_first = first_decay * first_moment + (1.0 - first_decay) * grad
    new_second = second_decay * second_moment + (1.0 - second_decay) * grad * grad
    new_weight = weight - learn_rate * (new_first / first_fix) / (
        jnp.sqrt(new_second / second_fix) + adam_eps
    )
    return (activated, feature_grad, new_weight, new_first, new_second)


def solution(mesh):
    return jax.shard_map(
        per_device,
        mesh=mesh,
        in_specs=(
            P("node", "feat", None),
            P("node", None, None),
            P("node"),
            P("node"),
            P("node"),
            P("feat", None),
            P("feat", None),
            P("feat", None),
            P("node", "feat", None),
        ),
        out_specs=(
            P("node", "feat", None),
            P("node", "feat", None),
            P("feat", None),
            P("feat", None),
            P("feat", None),
        ),
        check_vma=False,
    )
```

```python
import math

import jax
import jax.numpy as jnp
from jax import lax
from jax.sharding import PartitionSpec as P

REACH = 2


first_decay = 0.9
second_decay = 0.999
learn_rate = 0.05
first_fix = 1.0 - 0.9**10
second_fix = 1.0 - 0.999**10
adam_eps = 1e-08


def passed_along(block, axis, distance):
    devices = range(lax.axis_size(axis))
    route = [((i - distance) % len(devices), i) for i in devices]
    return lax.ppermute(block, axis, route)


def gathered_along(block, axis, dim, direct=False):
    size = lax.axis_size(axis)
    own = lax.axis_index(axis)
    width = block.shape[dim]
    if direct and not size & (size - 1):
        pieces = [(block, own)]
        for mask in range(1, size):
            route = [(i, i ^ mask) for i in range(size)]
            pieces.append((lax.ppermute(block, axis, route), own ^ mask))
    elif size & (size - 1):
        pieces = [(block, own)]
        for step in range(1, size):
            pieces.append((passed_along(block, axis, -step), (own + step) % size))
    else:
        pieces = [(block, own)]
        mask = size // 2
        while mask >= 1:
            held = jnp.stack([piece for piece, _ in pieces])
            got = lax.ppermute(held, axis, [(i, i ^ mask) for i in range(size)])
            pieces = pieces + [(got[k], index ^ mask) for k, (_, index) in enumerate(pieces)]
            mask //= 2
    shape = list(block.shape)
    shape[dim] = size * width
    whole = jnp.zeros(shape, block.dtype)
    for piece, index in pieces:
        whole = lax.dynamic_update_slice_in_dim(whole, piece, index * width, dim)
    return whole


def summed_over(block, axis):
    size = lax.axis_size(axis)
    if size & (size - 1):
        return lax.psum(block, axis)
    mask = 1
    while mask < size:
        block = block + lax.ppermute(block, axis, [(i, i ^ mask) for i in range(size)])
        mask *= 2
    return block


def summed_by_table(table, terms, spec):
    rounded = lax.reduce_precision(terms, exponent_bits=8, mantissa_bits=7)
    high = rounded.astype(jnp.bfloat16)
    low = (terms - rounded).astype(jnp.bfloat16)
    both = jnp.concatenate([high, low], axis=0)
    doubled = jnp.concatenate([table, table], axis=0).astype(jnp.bfloat16)
    return jnp.einsum(spec, doubled, both, preferred_element_type=jnp.float32)


def elu_slope(preact):
    return jnp.where(preact > 0, 1.0, jnp.exp(jnp.minimum(preact, 0.0)))


def one_hot_table(indices, count, dtype):
    return (indices[:, None] == jnp.arange(count)[None, :]).astype(dtype)


def per_device(
    features,
    tile_values,
    tile_row,
    tile_col,
    tile_count,
    weight,
    first_moment,
    second_moment,
    cotangent,
):
    cycle_size = lax.axis_size("node")
    own_node = lax.axis_index("node")
    blocks = features.shape[0]
    width_local = features.shape[1]
    tile_size = features.shape[2]
    slots = tile_values.shape[0]
    live = (jnp.arange(slots) < tile_count[0]).astype(jnp.float32)
    local_row = tile_row - own_node * blocks
    col_owner = tile_col // blocks
    col_block = tile_col % blocks
    offset = (col_owner - own_node) % cycle_size
    offset = jnp.where(offset > cycle_size // 2, offset - cycle_size, offset)
    source_slot = (offset + REACH) * blocks + col_block
    targets = (2 * REACH + 1) * blocks
    pick_source = one_hot_table(source_slot, targets, jnp.bfloat16)
    pick_row = one_hot_table(local_row, blocks, jnp.bfloat16)
    add_row = one_hot_table(local_row, blocks, jnp.float32) * live[:, None]
    add_source = one_hot_table(source_slot, targets, jnp.float32) * live[:, None]
    pieces = []
    for distance in range(-REACH, REACH + 1):
        if distance == 0:
            pieces.append(features)
        else:
            pieces.append(passed_along(features, "node", -distance))
    nearby = jnp.concatenate(pieces, axis=0)
    weight_half = weight.astype(jnp.bfloat16)
    packed = jnp.concatenate([cotangent, weight_half[None]], axis=0)
    packed_all = gathered_along(packed, "feat", 1, direct=True)
    cotangent_all = packed_all[:blocks]
    weight_all = packed_all[blocks]
    nearby, cotangent_all, weight_all = lax.optimization_barrier((nearby, cotangent_all, weight_all))
    sources = jnp.einsum(
        "ts,sfk->tfk", pick_source, nearby, preferred_element_type=jnp.float32
    ).astype(jnp.bfloat16)
    forward_terms = jnp.einsum(
        "tfk,tjk->tfj", sources, tile_values, preferred_element_type=jnp.float32
    )
    aggregate = summed_by_table(add_row, forward_terms, "tb,tfj->bfj")
    aggregate = aggregate.astype(jnp.bfloat16)
    aggregate_all = gathered_along(aggregate, "feat", 1)
    column_start = lax.axis_index("feat") * width_local
    preact = jnp.einsum(
        "bij,io->boj", aggregate_all, weight_all, preferred_element_type=jnp.float32
    )
    activated = lax.dynamic_slice_in_dim(jax.nn.elu(preact), column_start, width_local, 1)
    activated = activated.astype(jnp.bfloat16)
    slope_all = (cotangent_all.astype(jnp.float32) * elu_slope(preact)).astype(jnp.bfloat16)
    node_total = cycle_size * blocks * tile_size
    grad_local = jnp.einsum("bij,boj->io", aggregate, slope_all, preferred_element_type=jnp.float32)
    grad = summed_over(grad_local, "node") * (1.0 / math.sqrt(node_total))
    back_rows = jnp.einsum(
        "io,boj->bij", weight_half, slope_all, preferred_element_type=jnp.float32
    ).astype(jnp.bfloat16)
    back_sources = jnp.einsum(
        "tb,bfj->tfj", pick_row, back_rows, preferred_element_type=jnp.float32
    ).astype(jnp.bfloat16)
    back_terms = jnp.einsum(
        "tfj,tjk->tfk", back_sources, tile_values, preferred_element_type=jnp.float32
    )
    outgoing = summed_by_table(add_source, back_terms, "ts,tfk->sfk")
    outgoing = outgoing.reshape(2 * REACH + 1, blocks, width_local, tile_size)
    feature_grad = outgoing[REACH]
    for distance in range(-REACH, REACH + 1):
        if distance != 0:
            sent = outgoing[distance + REACH].astype(jnp.bfloat16)
            feature_grad = feature_grad + passed_along(sent, "node", distance).astype(jnp.float32)
    new_first = first_decay * first_moment + (1.0 - first_decay) * grad
    new_second = second_decay * second_moment + (1.0 - second_decay) * grad * grad
    new_weight = weight - learn_rate * (new_first / first_fix) / (
        jnp.sqrt(new_second / second_fix) + adam_eps
    )
    return (activated, feature_grad, new_weight, new_first, new_second)


def solution(mesh):
    return jax.shard_map(
        per_device,
        mesh=mesh,
        in_specs=(
            P("node", "feat", None),
            P("node", None, None),
            P("node"),
            P("node"),
            P("node"),
            P("feat", None),
            P("feat", None),
            P("feat", None),
            P("node", "feat", None),
        ),
        out_specs=(
            P("node", "feat", None),
            P("node", "feat", None),
            P("feat", None),
            P("feat", None),
            P("feat", None),
        ),
        check_vma=False,
    )
```

```python
import math

import jax
import jax.numpy as jnp
from jax import lax
from jax.sharding import PartitionSpec as P

REACH = 2


first_decay = 0.9
second_decay = 0.999
learn_rate = 0.05
first_fix = 1.0 - 0.9**10
second_fix = 1.0 - 0.999**10
adam_eps = 1e-08


def passed_along(block, axis, distance):
    devices = range(lax.axis_size(axis))
    route = [((i - distance) % len(devices), i) for i in devices]
    return lax.ppermute(block, axis, route)


def gathered_along(block, axis, dim):
    size = lax.axis_size(axis)
    own = lax.axis_index(axis)
    width = block.shape[dim]
    if size & (size - 1):
        pieces = [(block, own)]
        for step in range(1, size):
            pieces.append((passed_along(block, axis, -step), (own + step) % size))
    else:
        pieces = [(block, own)]
        mask = size // 2
        while mask >= 1:
            held = jnp.stack([piece for piece, _ in pieces])
            got = lax.ppermute(held, axis, [(i, i ^ mask) for i in range(size)])
            pieces = pieces + [(got[k], index ^ mask) for k, (_, index) in enumerate(pieces)]
            mask //= 2
    shape = list(block.shape)
    shape[dim] = size * width
    whole = jnp.zeros(shape, block.dtype)
    for piece, index in pieces:
        whole = lax.dynamic_update_slice_in_dim(whole, piece, index * width, dim)
    return whole


def summed_over(block, axis, beside=None):
    size = lax.axis_size(axis)
    if size & (size - 1):
        return lax.psum(block, axis), beside
    mask = 1
    while mask < size:
        block = block + lax.ppermute(block, axis, [(i, i ^ mask) for i in range(size)])
        if mask == 1 and beside is not None:
            block, beside = lax.optimization_barrier((block, beside))
        mask *= 2
    return block, beside


def summed_by_table(table, terms, spec):
    rounded = lax.reduce_precision(terms, exponent_bits=8, mantissa_bits=7)
    high = rounded.astype(jnp.bfloat16)
    low = (terms - rounded).astype(jnp.bfloat16)
    both = jnp.concatenate([high, low], axis=0)
    doubled = jnp.concatenate([table, table], axis=0).astype(jnp.bfloat16)
    return jnp.einsum(spec, doubled, both, preferred_element_type=jnp.float32)


def elu_slope(preact):
    return jnp.where(preact > 0, 1.0, jnp.exp(jnp.minimum(preact, 0.0)))


def one_hot_table(indices, count, dtype):
    return (indices[:, None] == jnp.arange(count)[None, :]).astype(dtype)


def per_device(
    features,
    tile_values,
    tile_row,
    tile_col,
    tile_count,
    weight,
    first_moment,
    second_moment,
    cotangent,
):
    cycle_size = lax.axis_size("node")
    own_node = lax.axis_index("node")
    blocks = features.shape[0]
    width_local = features.shape[1]
    tile_size = features.shape[2]
    slots = tile_values.shape[0]
    live = (jnp.arange(slots) < tile_count[0]).astype(jnp.float32)
    local_row = tile_row - own_node * blocks
    col_owner = tile_col // blocks
    col_block = tile_col % blocks
    offset = (col_owner - own_node) % cycle_size
    offset = jnp.where(offset > cycle_size // 2, offset - cycle_size, offset)
    source_slot = (offset + REACH) * blocks + col_block
    targets = (2 * REACH + 1) * blocks
    pick_source = one_hot_table(source_slot, targets, jnp.bfloat16)
    pick_row = one_hot_table(local_row, blocks, jnp.bfloat16)
    add_row = one_hot_table(local_row, blocks, jnp.float32) * live[:, None]
    add_source = one_hot_table(source_slot, targets, jnp.float32) * live[:, None]
    pieces = []
    for distance in range(-REACH, REACH + 1):
        if distance == 0:
            pieces.append(features)
        else:
            pieces.append(passed_along(features, "node", -distance))
    nearby = jnp.concatenate(pieces, axis=0)
    weight_half = weight.astype(jnp.bfloat16)
    packed = jnp.concatenate([cotangent, weight_half[None]], axis=0)
    packed_all = gathered_along(packed, "feat", 1)
    cotangent_all = packed_all[:blocks]
    weight_all = packed_all[blocks]
    nearby, cotangent_all, weight_all = lax.optimization_barrier((nearby, cotangent_all, weight_all))
    sources = jnp.einsum(
        "ts,sfk->tfk", pick_source, nearby, preferred_element_type=jnp.float32
    ).astype(jnp.bfloat16)
    forward_terms = jnp.einsum(
        "tfk,tjk->tfj", sources, tile_values, preferred_element_type=jnp.float32
    )
    aggregate = summed_by_table(add_row, forward_terms, "tb,tfj->bfj")
    aggregate = aggregate.astype(jnp.bfloat16)
    aggregate_all = gathered_along(aggregate, "feat", 1)
    column_start = lax.axis_index("feat") * width_local
    preact = jnp.einsum(
        "bij,io->boj", aggregate_all, weight_all, preferred_element_type=jnp.float32
    )
    activated = lax.dynamic_slice_in_dim(jax.nn.elu(preact), column_start, width_local, 1)
    activated = activated.astype(jnp.bfloat16)
    slope_all = (cotangent_all.astype(jnp.float32) * elu_slope(preact)).astype(jnp.bfloat16)
    node_total = cycle_size * blocks * tile_size
    grad_local = jnp.einsum("bij,boj->io", aggregate, slope_all, preferred_element_type=jnp.float32)
    grad, activated = summed_over(grad_local, "node", beside=activated)
    grad = grad * (1.0 / math.sqrt(node_total))
    back_rows = jnp.einsum(
        "io,boj->bij", weight_half, slope_all, preferred_element_type=jnp.float32
    ).astype(jnp.bfloat16)
    back_sources = jnp.einsum(
        "tb,bfj->tfj", pick_row, back_rows, preferred_element_type=jnp.float32
    ).astype(jnp.bfloat16)
    back_terms = jnp.einsum(
        "tfj,tjk->tfk", back_sources, tile_values, preferred_element_type=jnp.float32
    )
    outgoing = summed_by_table(add_source, back_terms, "ts,tfk->sfk")
    outgoing = outgoing.reshape(2 * REACH + 1, blocks, width_local, tile_size)
    feature_grad = outgoing[REACH]
    for distance in range(-REACH, REACH + 1):
        if distance != 0:
            sent = outgoing[distance + REACH].astype(jnp.bfloat16)
            feature_grad = feature_grad + passed_along(sent, "node", distance).astype(jnp.float32)
    new_first = first_decay * first_moment + (1.0 - first_decay) * grad
    new_second = second_decay * second_moment + (1.0 - second_decay) * grad * grad
    new_weight = weight - learn_rate * (new_first / first_fix) / (
        jnp.sqrt(new_second / second_fix) + adam_eps
    )
    return (activated, feature_grad, new_weight, new_first, new_second)


def solution(mesh):
    return jax.shard_map(
        per_device,
        mesh=mesh,
        in_specs=(
            P("node", "feat", None),
            P("node", None, None),
            P("node"),
            P("node"),
            P("node"),
            P("feat", None),
            P("feat", None),
            P("feat", None),
            P("node", "feat", None),
        ),
        out_specs=(
            P("node", "feat", None),
            P("node", "feat", None),
            P("feat", None),
            P("feat", None),
            P("feat", None),
        ),
        check_vma=False,
    )
```

```python
import math

import jax
import jax.numpy as jnp
from jax import lax
from jax.sharding import PartitionSpec as P

REACH = 2


first_decay = 0.9
second_decay = 0.999
learn_rate = 0.05
first_fix = 1.0 - 0.9**10
second_fix = 1.0 - 0.999**10
adam_eps = 1e-08


def passed_along(block, axis, distance):
    devices = range(lax.axis_size(axis))
    route = [((i - distance) % len(devices), i) for i in devices]
    return lax.ppermute(block, axis, route)


def gathered_along(block, axis, dim):
    size = lax.axis_size(axis)
    own = lax.axis_index(axis)
    width = block.shape[dim]
    if size & (size - 1):
        pieces = [(block, own)]
        for step in range(1, size):
            pieces.append((passed_along(block, axis, -step), (own + step) % size))
    else:
        pieces = [(block, own)]
        mask = size // 2
        while mask >= 1:
            held = jnp.stack([piece for piece, _ in pieces])
            got = lax.ppermute(held, axis, [(i, i ^ mask) for i in range(size)])
            pieces = pieces + [(got[k], index ^ mask) for k, (_, index) in enumerate(pieces)]
            mask //= 2
    shape = list(block.shape)
    shape[dim] = size * width
    whole = jnp.zeros(shape, block.dtype)
    for piece, index in pieces:
        whole = lax.dynamic_update_slice_in_dim(whole, piece, index * width, dim)
    return whole


def summed_over(block, axis, beside=None):
    size = lax.axis_size(axis)
    if size & (size - 1):
        return lax.psum(block, axis), beside
    own = lax.axis_index(axis)
    stride = 1
    while stride < size:
        if stride * 4 <= size:
            held = [block]
            for k in (1, 2, 3):
                route = [(i, i ^ (k * stride)) for i in range(size)]
                held.append(lax.ppermute(block, axis, route))
            held = jnp.stack(held)
            member = (own // stride) % 4
            ordered = [held[m ^ member] for m in range(4)]
            block = (ordered[0] + ordered[1]) + (ordered[2] + ordered[3])
            stride *= 4
        else:
            block = block + lax.ppermute(block, axis, [(i, i ^ stride) for i in range(size)])
            stride *= 2
        if beside is not None and stride <= 4:
            block, beside = lax.optimization_barrier((block, beside))
    return block, beside


def summed_by_table(table, terms, spec):
    rounded = lax.reduce_precision(terms, exponent_bits=8, mantissa_bits=7)
    high = rounded.astype(jnp.bfloat16)
    low = (terms - rounded).astype(jnp.bfloat16)
    both = jnp.concatenate([high, low], axis=0)
    doubled = jnp.concatenate([table, table], axis=0).astype(jnp.bfloat16)
    return jnp.einsum(spec, doubled, both, preferred_element_type=jnp.float32)


def elu_slope(preact):
    return jnp.where(preact > 0, 1.0, jnp.exp(jnp.minimum(preact, 0.0)))


def one_hot_table(indices, count, dtype):
    return (indices[:, None] == jnp.arange(count)[None, :]).astype(dtype)


def per_device(
    features,
    tile_values,
    tile_row,
    tile_col,
    tile_count,
    weight,
    first_moment,
    second_moment,
    cotangent,
):
    cycle_size = lax.axis_size("node")
    own_node = lax.axis_index("node")
    blocks = features.shape[0]
    width_local = features.shape[1]
    tile_size = features.shape[2]
    slots = tile_values.shape[0]
    live = (jnp.arange(slots) < tile_count[0]).astype(jnp.float32)
    local_row = tile_row - own_node * blocks
    col_owner = tile_col // blocks
    col_block = tile_col % blocks
    offset = (col_owner - own_node) % cycle_size
    offset = jnp.where(offset > cycle_size // 2, offset - cycle_size, offset)
    source_slot = (offset + REACH) * blocks + col_block
    targets = (2 * REACH + 1) * blocks
    pick_source = one_hot_table(source_slot, targets, jnp.bfloat16)
    pick_row = one_hot_table(local_row, blocks, jnp.bfloat16)
    add_row = one_hot_table(local_row, blocks, jnp.float32) * live[:, None]
    add_source = one_hot_table(source_slot, targets, jnp.float32) * live[:, None]
    pieces = []
    for distance in range(-REACH, REACH + 1):
        if distance == 0:
            pieces.append(features)
        else:
            pieces.append(passed_along(features, "node", -distance))
    nearby = jnp.concatenate(pieces, axis=0)
    weight_half = weight.astype(jnp.bfloat16)
    packed = jnp.concatenate([cotangent, weight_half[None]], axis=0)
    packed_all = gathered_along(packed, "feat", 1)
    cotangent_all = packed_all[:blocks]
    weight_all = packed_all[blocks]
    nearby, cotangent_all, weight_all = lax.optimization_barrier((nearby, cotangent_all, weight_all))
    sources = jnp.einsum(
        "ts,sfk->tfk", pick_source, nearby, preferred_element_type=jnp.float32
    ).astype(jnp.bfloat16)
    forward_terms = jnp.einsum(
        "tfk,tjk->tfj", sources, tile_values, preferred_element_type=jnp.float32
    )
    aggregate = summed_by_table(add_row, forward_terms, "tb,tfj->bfj")
    aggregate = aggregate.astype(jnp.bfloat16)
    aggregate_all = gathered_along(aggregate, "feat", 1)
    column_start = lax.axis_index("feat") * width_local
    preact = jnp.einsum(
        "bij,io->boj", aggregate_all, weight_all, preferred_element_type=jnp.float32
    )
    activated = lax.dynamic_slice_in_dim(jax.nn.elu(preact), column_start, width_local, 1)
    activated = activated.astype(jnp.bfloat16)
    slope_all = (cotangent_all.astype(jnp.float32) * elu_slope(preact)).astype(jnp.bfloat16)
    node_total = cycle_size * blocks * tile_size
    grad_local = jnp.einsum("bij,boj->io", aggregate, slope_all, preferred_element_type=jnp.float32)
    grad, activated = summed_over(grad_local, "node", beside=activated)
    grad = grad * (1.0 / math.sqrt(node_total))
    back_rows = jnp.einsum(
        "io,boj->bij", weight_half, slope_all, preferred_element_type=jnp.float32
    ).astype(jnp.bfloat16)
    back_sources = jnp.einsum(
        "tb,bfj->tfj", pick_row, back_rows, preferred_element_type=jnp.float32
    ).astype(jnp.bfloat16)
    back_terms = jnp.einsum(
        "tfj,tjk->tfk", back_sources, tile_values, preferred_element_type=jnp.float32
    )
    outgoing = summed_by_table(add_source, back_terms, "ts,tfk->sfk")
    outgoing = outgoing.reshape(2 * REACH + 1, blocks, width_local, tile_size)
    feature_grad = outgoing[REACH]
    for distance in range(-REACH, REACH + 1):
        if distance != 0:
            sent = outgoing[distance + REACH].astype(jnp.bfloat16)
            feature_grad = feature_grad + passed_along(sent, "node", distance).astype(jnp.float32)
    new_first = first_decay * first_moment + (1.0 - first_decay) * grad
    new_second = second_decay * second_moment + (1.0 - second_decay) * grad * grad
    new_weight = weight - learn_rate * (new_first / first_fix) / (
        jnp.sqrt(new_second / second_fix) + adam_eps
    )
    return (activated, feature_grad, new_weight, new_first, new_second)


def solution(mesh):
    return jax.shard_map(
        per_device,
        mesh=mesh,
        in_specs=(
            P("node", "feat", None),
            P("node", None, None),
            P("node"),
            P("node"),
            P("node"),
            P("feat", None),
            P("feat", None),
            P("feat", None),
            P("node", "feat", None),
        ),
        out_specs=(
            P("node", "feat", None),
            P("node", "feat", None),
            P("feat", None),
            P("feat", None),
            P("feat", None),
        ),
        check_vma=False,
    )
```

```python
import math

import jax
import jax.numpy as jnp
from jax import lax
from jax.sharding import PartitionSpec as P

REACH = 2


first_decay = 0.9
second_decay = 0.999
learn_rate = 0.05
first_fix = 1.0 - 0.9**10
second_fix = 1.0 - 0.999**10
adam_eps = 1e-08


def passed_along(block, axis, distance):
    devices = range(lax.axis_size(axis))
    route = [((i - distance) % len(devices), i) for i in devices]
    return lax.ppermute(block, axis, route)


def gathered_along(block, axis, dim):
    size = lax.axis_size(axis)
    own = lax.axis_index(axis)
    width = block.shape[dim]
    if size & (size - 1):
        pieces = [(block, own)]
        for step in range(1, size):
            pieces.append((passed_along(block, axis, -step), (own + step) % size))
    else:
        pieces = [(block, own)]
        mask = size // 2
        while mask >= 1:
            held = jnp.stack([piece for piece, _ in pieces])
            got = lax.ppermute(held, axis, [(i, i ^ mask) for i in range(size)])
            pieces = pieces + [(got[k], index ^ mask) for k, (_, index) in enumerate(pieces)]
            mask //= 2
    shape = list(block.shape)
    shape[dim] = size * width
    whole = jnp.zeros(shape, block.dtype)
    for piece, index in pieces:
        whole = lax.dynamic_update_slice_in_dim(whole, piece, index * width, dim)
    return whole


def summed_over(block, axis, first=1, last=None):
    size = lax.axis_size(axis)
    if size & (size - 1):
        return lax.psum(block, axis) if first == 1 else block
    last = size if last is None else min(last, size)
    own = lax.axis_index(axis)
    stride = first
    while stride < last:
        if stride * 4 <= last:
            held = [block]
            for k in (1, 2, 3):
                route = [(i, i ^ (k * stride)) for i in range(size)]
                held.append(lax.ppermute(block, axis, route))
            held = jnp.stack(held)
            member = (own // stride) % 4
            ordered = [held[m ^ member] for m in range(4)]
            block = (ordered[0] + ordered[1]) + (ordered[2] + ordered[3])
            stride *= 4
        else:
            block = block + lax.ppermute(block, axis, [(i, i ^ stride) for i in range(size)])
            stride *= 2
    return block


def summed_by_table(table, terms, spec):
    rounded = lax.reduce_precision(terms, exponent_bits=8, mantissa_bits=7)
    high = rounded.astype(jnp.bfloat16)
    low = (terms - rounded).astype(jnp.bfloat16)
    both = jnp.concatenate([high, low], axis=0)
    doubled = jnp.concatenate([table, table], axis=0).astype(jnp.bfloat16)
    return jnp.einsum(spec, doubled, both, preferred_element_type=jnp.float32)


def elu_slope(preact):
    return jnp.where(preact > 0, 1.0, jnp.exp(jnp.minimum(preact, 0.0)))


def one_hot_table(indices, count, dtype):
    return (indices[:, None] == jnp.arange(count)[None, :]).astype(dtype)


def per_device(
    features,
    tile_values,
    tile_row,
    tile_col,
    tile_count,
    weight,
    first_moment,
    second_moment,
    cotangent,
):
    cycle_size = lax.axis_size("node")
    own_node = lax.axis_index("node")
    blocks = features.shape[0]
    width_local = features.shape[1]
    tile_size = features.shape[2]
    slots = tile_values.shape[0]
    live = (jnp.arange(slots) < tile_count[0]).astype(jnp.float32)
    local_row = tile_row - own_node * blocks
    col_owner = tile_col // blocks
    col_block = tile_col % blocks
    offset = (col_owner - own_node) % cycle_size
    offset = jnp.where(offset > cycle_size // 2, offset - cycle_size, offset)
    source_slot = (offset + REACH) * blocks + col_block
    targets = (2 * REACH + 1) * blocks
    pick_source = one_hot_table(source_slot, targets, jnp.bfloat16)
    pick_row = one_hot_table(local_row, blocks, jnp.bfloat16)
    add_row = one_hot_table(local_row, blocks, jnp.float32) * live[:, None]
    add_source = one_hot_table(source_slot, targets, jnp.float32) * live[:, None]
    pieces = []
    for distance in range(-REACH, REACH + 1):
        if distance == 0:
            pieces.append(features)
        else:
            pieces.append(passed_along(features, "node", -distance))
    nearby = jnp.concatenate(pieces, axis=0)
    weight_half = weight.astype(jnp.bfloat16)
    packed = jnp.concatenate([cotangent, weight_half[None]], axis=0)
    packed_all = gathered_along(packed, "feat", 1)
    cotangent_all = packed_all[:blocks]
    weight_all = packed_all[blocks]
    nearby, cotangent_all, weight_all = lax.optimization_barrier((nearby, cotangent_all, weight_all))
    sources = jnp.einsum(
        "ts,sfk->tfk", pick_source, nearby, preferred_element_type=jnp.float32
    ).astype(jnp.bfloat16)
    forward_terms = jnp.einsum(
        "tfk,tjk->tfj", sources, tile_values, preferred_element_type=jnp.float32
    )
    aggregate = summed_by_table(add_row, forward_terms, "tb,tfj->bfj")
    aggregate = aggregate.astype(jnp.bfloat16)
    aggregate_all = gathered_along(aggregate, "feat", 1)
    column_start = lax.axis_index("feat") * width_local
    preact = jnp.einsum(
        "bij,io->boj", aggregate_all, weight_all, preferred_element_type=jnp.float32
    )
    activated = lax.dynamic_slice_in_dim(jax.nn.elu(preact), column_start, width_local, 1)
    activated = activated.astype(jnp.bfloat16)
    slope_all = (cotangent_all.astype(jnp.float32) * elu_slope(preact)).astype(jnp.bfloat16)
    node_total = cycle_size * blocks * tile_size
    grad_local = jnp.einsum("bij,boj->io", aggregate, slope_all, preferred_element_type=jnp.float32)
    grad_partial = summed_over(grad_local, "node", last=4)
    back_rows = jnp.einsum(
        "io,boj->bij", weight_half, slope_all, preferred_element_type=jnp.float32
    ).astype(jnp.bfloat16)
    back_sources = jnp.einsum(
        "tb,bfj->tfj", pick_row, back_rows, preferred_element_type=jnp.float32
    ).astype(jnp.bfloat16)
    back_terms = jnp.einsum(
        "tfj,tjk->tfk", back_sources, tile_values, preferred_element_type=jnp.float32
    )
    outgoing = summed_by_table(add_source, back_terms, "ts,tfk->sfk")
    outgoing = outgoing.reshape(2 * REACH + 1, blocks, width_local, tile_size)
    feature_grad = outgoing[REACH]
    received = []
    for distance in range(-REACH, REACH + 1):
        if distance != 0:
            sent = outgoing[distance + REACH].astype(jnp.bfloat16)
            received.append(passed_along(sent, "node", distance))
    grad_partial, activated, received[0] = lax.optimization_barrier(
        (grad_partial, activated, received[0])
    )
    grad = summed_over(grad_partial, "node", first=4) * (1.0 / math.sqrt(node_total))
    for piece in received:
        feature_grad = feature_grad + piece.astype(jnp.float32)
    new_first = first_decay * first_moment + (1.0 - first_decay) * grad
    new_second = second_decay * second_moment + (1.0 - second_decay) * grad * grad
    new_weight = weight - learn_rate * (new_first / first_fix) / (
        jnp.sqrt(new_second / second_fix) + adam_eps
    )
    return (activated, feature_grad, new_weight, new_first, new_second)


def solution(mesh):
    return jax.shard_map(
        per_device,
        mesh=mesh,
        in_specs=(
            P("node", "feat", None),
            P("node", None, None),
            P("node"),
            P("node"),
            P("node"),
            P("feat", None),
            P("feat", None),
            P("feat", None),
            P("node", "feat", None),
        ),
        out_specs=(
            P("node", "feat", None),
            P("node", "feat", None),
            P("feat", None),
            P("feat", None),
            P("feat", None),
        ),
        check_vma=False,
    )
```

```python
import math

import jax
import jax.numpy as jnp
from jax import lax
from jax.sharding import PartitionSpec as P

REACH = 2


first_decay = 0.9
second_decay = 0.999
learn_rate = 0.05
first_fix = 1.0 - 0.9**10
second_fix = 1.0 - 0.999**10
adam_eps = 1e-08


def passed_along(block, axis, distance):
    devices = range(lax.axis_size(axis))
    route = [((i - distance) % len(devices), i) for i in devices]
    return lax.ppermute(block, axis, route)


def gathered_along(block, axis, dim):
    size = lax.axis_size(axis)
    own = lax.axis_index(axis)
    width = block.shape[dim]
    if size & (size - 1):
        pieces = [(block, own)]
        for step in range(1, size):
            pieces.append((passed_along(block, axis, -step), (own + step) % size))
    else:
        pieces = [(block, own)]
        mask = size // 2
        while mask >= 1:
            held = jnp.stack([piece for piece, _ in pieces])
            got = lax.ppermute(held, axis, [(i, i ^ mask) for i in range(size)])
            pieces = pieces + [(got[k], index ^ mask) for k, (_, index) in enumerate(pieces)]
            mask //= 2
    shape = list(block.shape)
    shape[dim] = size * width
    whole = jnp.zeros(shape, block.dtype)
    for piece, index in pieces:
        whole = lax.dynamic_update_slice_in_dim(whole, piece, index * width, dim)
    return whole


def summed_over(block, axis, first=1, last=None):
    size = lax.axis_size(axis)
    if size & (size - 1):
        return lax.psum(block, axis) if first == 1 else block
    last = size if last is None else min(last, size)
    own = lax.axis_index(axis)
    stride = first
    while stride < last:
        if stride * 4 <= last:
            held = [block]
            for k in (1, 2, 3):
                route = [(i, i ^ (k * stride)) for i in range(size)]
                held.append(lax.ppermute(block, axis, route))
            held = jnp.stack(held)
            member = (own // stride) % 4
            ordered = [held[m ^ member] for m in range(4)]
            block = (ordered[0] + ordered[1]) + (ordered[2] + ordered[3])
            stride *= 4
        else:
            block = block + lax.ppermute(block, axis, [(i, i ^ stride) for i in range(size)])
            stride *= 2
    return block


def summed_by_table(table, terms, spec):
    rounded = lax.reduce_precision(terms, exponent_bits=8, mantissa_bits=7)
    high = rounded.astype(jnp.bfloat16)
    low = (terms - rounded).astype(jnp.bfloat16)
    both = jnp.concatenate([high, low], axis=0)
    doubled = jnp.concatenate([table, table], axis=0).astype(jnp.bfloat16)
    return jnp.einsum(spec, doubled, both, preferred_element_type=jnp.float32)


def elu_slope(preact):
    return jnp.where(preact > 0, 1.0, jnp.exp(jnp.minimum(preact, 0.0)))


def one_hot_table(indices, count, dtype):
    return (indices[:, None] == jnp.arange(count)[None, :]).astype(dtype)


def per_device(
    features,
    tile_values,
    tile_row,
    tile_col,
    tile_count,
    weight,
    first_moment,
    second_moment,
    cotangent,
):
    cycle_size = lax.axis_size("node")
    own_node = lax.axis_index("node")
    blocks = features.shape[0]
    width_local = features.shape[1]
    tile_size = features.shape[2]
    slots = tile_values.shape[0]
    live = (jnp.arange(slots) < tile_count[0]).astype(jnp.float32)
    local_row = tile_row - own_node * blocks
    col_owner = tile_col // blocks
    col_block = tile_col % blocks
    offset = (col_owner - own_node) % cycle_size
    offset = jnp.where(offset > cycle_size // 2, offset - cycle_size, offset)
    source_slot = (offset + REACH) * blocks + col_block
    targets = (2 * REACH + 1) * blocks
    pick_source = one_hot_table(source_slot, targets, jnp.bfloat16)
    pick_row = one_hot_table(local_row, blocks, jnp.bfloat16)
    add_row = one_hot_table(local_row, blocks, jnp.float32) * live[:, None]
    add_source = one_hot_table(source_slot, targets, jnp.float32) * live[:, None]
    pieces = []
    for distance in range(-REACH, REACH + 1):
        if distance == 0:
            pieces.append(features)
        else:
            pieces.append(passed_along(features, "node", -distance))
    nearby = jnp.concatenate(pieces, axis=0)
    weight_half = weight.astype(jnp.bfloat16)
    packed = jnp.concatenate([cotangent, weight_half[None]], axis=0)
    packed_all = gathered_along(packed, "feat", 1)
    cotangent_all = packed_all[:blocks]
    weight_all = packed_all[blocks]
    nearby, cotangent_all, weight_all = lax.optimization_barrier((nearby, cotangent_all, weight_all))
    sources = jnp.einsum(
        "ts,sfk->tfk", pick_source, nearby, preferred_element_type=jnp.float32
    ).astype(jnp.bfloat16)
    forward_terms = jnp.einsum(
        "tfk,tjk->tfj", sources, tile_values, preferred_element_type=jnp.float32
    )
    aggregate = summed_by_table(add_row, forward_terms, "tb,tfj->bfj")
    aggregate = aggregate.astype(jnp.bfloat16)
    aggregate_all = gathered_along(aggregate, "feat", 1)
    column_start = lax.axis_index("feat") * width_local
    preact = jnp.einsum(
        "bij,io->boj", aggregate_all, weight_all, preferred_element_type=jnp.float32
    )
    preact_local = lax.dynamic_slice_in_dim(preact, column_start, width_local, 1)
    slope_all = (cotangent_all.astype(jnp.float32) * elu_slope(preact)).astype(jnp.bfloat16)
    node_total = cycle_size * blocks * tile_size
    grad_local = jnp.einsum("bij,boj->io", aggregate, slope_all, preferred_element_type=jnp.float32)
    grad_partial = summed_over(grad_local, "node", last=4)
    back_rows = jnp.einsum(
        "io,boj->bij", weight_half, slope_all, preferred_element_type=jnp.float32
    ).astype(jnp.bfloat16)
    back_sources = jnp.einsum(
        "tb,bfj->tfj", pick_row, back_rows, preferred_element_type=jnp.float32
    ).astype(jnp.bfloat16)
    back_terms = jnp.einsum(
        "tfj,tjk->tfk", back_sources, tile_values, preferred_element_type=jnp.float32
    )
    outgoing = summed_by_table(add_source, back_terms, "ts,tfk->sfk")
    outgoing = outgoing.reshape(2 * REACH + 1, blocks, width_local, tile_size)
    feature_grad = outgoing[REACH]
    received = []
    for distance in range(-REACH, REACH + 1):
        if distance != 0:
            sent = outgoing[distance + REACH].astype(jnp.bfloat16)
            received.append(passed_along(sent, "node", distance))
    grad_partial, preact_local, received[0] = lax.optimization_barrier(
        (grad_partial, preact_local, received[0])
    )
    activated = jax.nn.elu(preact_local).astype(jnp.bfloat16)
    grad = summed_over(grad_partial, "node", first=4) * (1.0 / math.sqrt(node_total))
    for piece in received:
        feature_grad = feature_grad + piece.astype(jnp.float32)
    new_first = first_decay * first_moment + (1.0 - first_decay) * grad
    new_second = second_decay * second_moment + (1.0 - second_decay) * grad * grad
    new_weight = weight - learn_rate * (new_first / first_fix) / (
        jnp.sqrt(new_second / second_fix) + adam_eps
    )
    return (activated, feature_grad, new_weight, new_first, new_second)


def solution(mesh):
    return jax.shard_map(
        per_device,
        mesh=mesh,
        in_specs=(
            P("node", "feat", None),
            P("node", None, None),
            P("node"),
            P("node"),
            P("node"),
            P("feat", None),
            P("feat", None),
            P("feat", None),
            P("node", "feat", None),
        ),
        out_specs=(
            P("node", "feat", None),
            P("node", "feat", None),
            P("feat", None),
            P("feat", None),
            P("feat", None),
        ),
        check_vma=False,
    )
```

```python
import math

import jax
import jax.numpy as jnp
from jax import lax
from jax.sharding import PartitionSpec as P

REACH = 2


first_decay = 0.9
second_decay = 0.999
learn_rate = 0.05
first_fix = 1.0 - 0.9**10
second_fix = 1.0 - 0.999**10
adam_eps = 1e-08


def passed_along(block, axis, distance):
    devices = range(lax.axis_size(axis))
    route = [((i - distance) % len(devices), i) for i in devices]
    return lax.ppermute(block, axis, route)


def gathered_along(block, axis, dim, beside=None):
    size = lax.axis_size(axis)
    own = lax.axis_index(axis)
    width = block.shape[dim]
    if size & (size - 1):
        pieces = [(block, own)]
        for step in range(1, size):
            pieces.append((passed_along(block, axis, -step), (own + step) % size))
    else:
        pieces = [(block, own)]
        mask = size // 2
        while mask >= 1:
            held = jnp.stack([piece for piece, _ in pieces])
            got = lax.ppermute(held, axis, [(i, i ^ mask) for i in range(size)])
            if beside is not None and mask == size // 2:
                got, beside = lax.optimization_barrier((got, beside))
            pieces = pieces + [(got[k], index ^ mask) for k, (_, index) in enumerate(pieces)]
            mask //= 2
    shape = list(block.shape)
    shape[dim] = size * width
    whole = jnp.zeros(shape, block.dtype)
    for piece, index in pieces:
        whole = lax.dynamic_update_slice_in_dim(whole, piece, index * width, dim)
    if beside is None:
        return whole
    return whole, beside


def summed_over(block, axis, first=1, last=None):
    size = lax.axis_size(axis)
    if size & (size - 1):
        return lax.psum(block, axis) if first == 1 else block
    last = size if last is None else min(last, size)
    own = lax.axis_index(axis)
    stride = first
    while stride < last:
        if stride * 4 <= last:
            held = [block]
            for k in (1, 2, 3):
                route = [(i, i ^ (k * stride)) for i in range(size)]
                held.append(lax.ppermute(block, axis, route))
            held = jnp.stack(held)
            member = (own // stride) % 4
            ordered = [held[m ^ member] for m in range(4)]
            block = (ordered[0] + ordered[1]) + (ordered[2] + ordered[3])
            stride *= 4
        else:
            block = block + lax.ppermute(block, axis, [(i, i ^ stride) for i in range(size)])
            stride *= 2
    return block


def summed_by_table(table, terms, spec):
    rounded = lax.reduce_precision(terms, exponent_bits=8, mantissa_bits=7)
    high = rounded.astype(jnp.bfloat16)
    low = (terms - rounded).astype(jnp.bfloat16)
    both = jnp.concatenate([high, low], axis=0)
    doubled = jnp.concatenate([table, table], axis=0).astype(jnp.bfloat16)
    return jnp.einsum(spec, doubled, both, preferred_element_type=jnp.float32)


def elu_slope(preact):
    return jnp.where(preact > 0, 1.0, jnp.exp(jnp.minimum(preact, 0.0)))


def one_hot_table(indices, count, dtype):
    return (indices[:, None] == jnp.arange(count)[None, :]).astype(dtype)


def per_device(
    features,
    tile_values,
    tile_row,
    tile_col,
    tile_count,
    weight,
    first_moment,
    second_moment,
    cotangent,
):
    cycle_size = lax.axis_size("node")
    own_node = lax.axis_index("node")
    blocks = features.shape[0]
    width_local = features.shape[1]
    tile_size = features.shape[2]
    slots = tile_values.shape[0]
    live = (jnp.arange(slots) < tile_count[0]).astype(jnp.float32)
    local_row = tile_row - own_node * blocks
    col_owner = tile_col // blocks
    col_block = tile_col % blocks
    offset = (col_owner - own_node) % cycle_size
    offset = jnp.where(offset > cycle_size // 2, offset - cycle_size, offset)
    source_slot = (offset + REACH) * blocks + col_block
    targets = (2 * REACH + 1) * blocks
    pick_source = one_hot_table(source_slot, targets, jnp.bfloat16)
    pick_row = one_hot_table(local_row, blocks, jnp.bfloat16)
    add_row = one_hot_table(local_row, blocks, jnp.float32) * live[:, None]
    add_source = one_hot_table(source_slot, targets, jnp.float32) * live[:, None]
    pieces = []
    for distance in range(-REACH, REACH + 1):
        if distance == 0:
            pieces.append(features)
        else:
            pieces.append(passed_along(features, "node", -distance))
    nearby = jnp.concatenate(pieces, axis=0)
    weight_half = weight.astype(jnp.bfloat16)
    packed = jnp.concatenate([cotangent, weight_half[None]], axis=0)
    packed_all, nearby = gathered_along(packed, "feat", 1, beside=nearby)
    cotangent_all = packed_all[:blocks]
    weight_all = packed_all[blocks]
    sources = jnp.einsum(
        "ts,sfk->tfk", pick_source, nearby, preferred_element_type=jnp.float32
    ).astype(jnp.bfloat16)
    forward_terms = jnp.einsum(
        "tfk,tjk->tfj", sources, tile_values, preferred_element_type=jnp.float32
    )
    aggregate = summed_by_table(add_row, forward_terms, "tb,tfj->bfj")
    aggregate = aggregate.astype(jnp.bfloat16)
    aggregate_all = gathered_along(aggregate, "feat", 1)
    column_start = lax.axis_index("feat") * width_local
    preact = jnp.einsum(
        "bij,io->boj", aggregate_all, weight_all, preferred_element_type=jnp.float32
    )
    activated = lax.dynamic_slice_in_dim(jax.nn.elu(preact), column_start, width_local, 1)
    activated = activated.astype(jnp.bfloat16)
    slope_all = (cotangent_all.astype(jnp.float32) * elu_slope(preact)).astype(jnp.bfloat16)
    node_total = cycle_size * blocks * tile_size
    grad_local = jnp.einsum("bij,boj->io", aggregate, slope_all, preferred_element_type=jnp.float32)
    grad_partial = summed_over(grad_local, "node", last=4)
    back_rows = jnp.einsum(
        "io,boj->bij", weight_half, slope_all, preferred_element_type=jnp.float32
    ).astype(jnp.bfloat16)
    back_sources = jnp.einsum(
        "tb,bfj->tfj", pick_row, back_rows, preferred_element_type=jnp.float32
    ).astype(jnp.bfloat16)
    back_terms = jnp.einsum(
        "tfj,tjk->tfk", back_sources, tile_values, preferred_element_type=jnp.float32
    )
    outgoing = summed_by_table(add_source, back_terms, "ts,tfk->sfk")
    outgoing = outgoing.reshape(2 * REACH + 1, blocks, width_local, tile_size)
    feature_grad = outgoing[REACH]
    received = []
    for distance in range(-REACH, REACH + 1):
        if distance != 0:
            sent = outgoing[distance + REACH].astype(jnp.bfloat16)
            received.append(passed_along(sent, "node", distance))
    grad_partial, activated, received[0] = lax.optimization_barrier(
        (grad_partial, activated, received[0])
    )
    grad = summed_over(grad_partial, "node", first=4) * (1.0 / math.sqrt(node_total))
    for piece in received:
        feature_grad = feature_grad + piece.astype(jnp.float32)
    new_first = first_decay * first_moment + (1.0 - first_decay) * grad
    new_second = second_decay * second_moment + (1.0 - second_decay) * grad * grad
    new_weight = weight - learn_rate * (new_first / first_fix) / (
        jnp.sqrt(new_second / second_fix) + adam_eps
    )
    return (activated, feature_grad, new_weight, new_first, new_second)


def solution(mesh):
    return jax.shard_map(
        per_device,
        mesh=mesh,
        in_specs=(
            P("node", "feat", None),
            P("node", None, None),
            P("node"),
            P("node"),
            P("node"),
            P("feat", None),
            P("feat", None),
            P("feat", None),
            P("node", "feat", None),
        ),
        out_specs=(
            P("node", "feat", None),
            P("node", "feat", None),
            P("feat", None),
            P("feat", None),
            P("feat", None),
        ),
        check_vma=False,
    )
```

```python
import math

import jax
import jax.numpy as jnp
from jax import lax
from jax.sharding import PartitionSpec as P

REACH = 2


first_decay = 0.9
second_decay = 0.999
learn_rate = 0.05
first_fix = 1.0 - 0.9**10
second_fix = 1.0 - 0.999**10
adam_eps = 1e-08


def passed_along(block, axis, distance):
    devices = range(lax.axis_size(axis))
    route = [((i - distance) % len(devices), i) for i in devices]
    return lax.ppermute(block, axis, route)


def gathered_along(block, axis, dim, direct=False):
    size = lax.axis_size(axis)
    own = lax.axis_index(axis)
    width = block.shape[dim]
    if direct and not size & (size - 1):
        pieces = [(block, own)]
        for mask in range(1, size):
            route = [(i, i ^ mask) for i in range(size)]
            pieces.append((lax.ppermute(block, axis, route), own ^ mask))
    elif size & (size - 1):
        pieces = [(block, own)]
        for step in range(1, size):
            pieces.append((passed_along(block, axis, -step), (own + step) % size))
    else:
        pieces = [(block, own)]
        mask = size // 2
        while mask >= 1:
            held = jnp.stack([piece for piece, _ in pieces])
            got = lax.ppermute(held, axis, [(i, i ^ mask) for i in range(size)])
            pieces = pieces + [(got[k], index ^ mask) for k, (_, index) in enumerate(pieces)]
            mask //= 2
    shape = list(block.shape)
    shape[dim] = size * width
    whole = jnp.zeros(shape, block.dtype)
    for piece, index in pieces:
        whole = lax.dynamic_update_slice_in_dim(whole, piece, index * width, dim)
    return whole


def summed_over(block, axis, first=1, last=None):
    size = lax.axis_size(axis)
    if size & (size - 1):
        return lax.psum(block, axis) if first == 1 else block
    last = size if last is None else min(last, size)
    own = lax.axis_index(axis)
    stride = first
    while stride < last:
        if stride * 4 <= last:
            held = [block]
            for k in (1, 2, 3):
                route = [(i, i ^ (k * stride)) for i in range(size)]
                held.append(lax.ppermute(block, axis, route))
            held = jnp.stack(held)
            member = (own // stride) % 4
            ordered = [held[m ^ member] for m in range(4)]
            block = (ordered[0] + ordered[1]) + (ordered[2] + ordered[3])
            stride *= 4
        else:
            block = block + lax.ppermute(block, axis, [(i, i ^ stride) for i in range(size)])
            stride *= 2
    return block


def summed_by_table(table, terms, spec):
    rounded = lax.reduce_precision(terms, exponent_bits=8, mantissa_bits=7)
    high = rounded.astype(jnp.bfloat16)
    low = (terms - rounded).astype(jnp.bfloat16)
    both = jnp.concatenate([high, low], axis=0)
    doubled = jnp.concatenate([table, table], axis=0).astype(jnp.bfloat16)
    return jnp.einsum(spec, doubled, both, preferred_element_type=jnp.float32)


def elu_slope(preact):
    return jnp.where(preact > 0, 1.0, jnp.exp(jnp.minimum(preact, 0.0)))


def one_hot_table(indices, count, dtype):
    return (indices[:, None] == jnp.arange(count)[None, :]).astype(dtype)


def per_device(
    features,
    tile_values,
    tile_row,
    tile_col,
    tile_count,
    weight,
    first_moment,
    second_moment,
    cotangent,
):
    cycle_size = lax.axis_size("node")
    own_node = lax.axis_index("node")
    blocks = features.shape[0]
    width_local = features.shape[1]
    tile_size = features.shape[2]
    slots = tile_values.shape[0]
    live = (jnp.arange(slots) < tile_count[0]).astype(jnp.float32)
    local_row = tile_row - own_node * blocks
    col_owner = tile_col // blocks
    col_block = tile_col % blocks
    offset = (col_owner - own_node) % cycle_size
    offset = jnp.where(offset > cycle_size // 2, offset - cycle_size, offset)
    source_slot = (offset + REACH) * blocks + col_block
    targets = (2 * REACH + 1) * blocks
    pick_source = one_hot_table(source_slot, targets, jnp.bfloat16)
    pick_row = one_hot_table(local_row, blocks, jnp.bfloat16)
    add_row = one_hot_table(local_row, blocks, jnp.float32) * live[:, None]
    add_source = one_hot_table(source_slot, targets, jnp.float32) * live[:, None]
    pieces = []
    for distance in range(-REACH, REACH + 1):
        if distance == 0:
            pieces.append(features)
        else:
            pieces.append(passed_along(features, "node", -distance))
    nearby = jnp.concatenate(pieces, axis=0)
    weight_half = weight.astype(jnp.bfloat16)
    packed = jnp.concatenate([cotangent, weight_half[None]], axis=0)
    packed_all = gathered_along(packed, "feat", 1)
    cotangent_all = packed_all[:blocks]
    weight_all = packed_all[blocks]
    nearby, cotangent_all, weight_all = lax.optimization_barrier((nearby, cotangent_all, weight_all))
    sources = jnp.einsum(
        "ts,sfk->tfk", pick_source, nearby, preferred_element_type=jnp.float32
    ).astype(jnp.bfloat16)
    forward_terms = jnp.einsum(
        "tfk,tjk->tfj", sources, tile_values, preferred_element_type=jnp.float32
    )
    aggregate = summed_by_table(add_row, forward_terms, "tb,tfj->bfj")
    aggregate = aggregate.astype(jnp.bfloat16)
    aggregate_all = gathered_along(aggregate, "feat", 1, direct=True)
    column_start = lax.axis_index("feat") * width_local
    preact = jnp.einsum(
        "bij,io->boj", aggregate_all, weight_all, preferred_element_type=jnp.float32
    )
    activated = lax.dynamic_slice_in_dim(jax.nn.elu(preact), column_start, width_local, 1)
    activated = activated.astype(jnp.bfloat16)
    slope_all = (cotangent_all.astype(jnp.float32) * elu_slope(preact)).astype(jnp.bfloat16)
    node_total = cycle_size * blocks * tile_size
    grad_local = jnp.einsum("bij,boj->io", aggregate, slope_all, preferred_element_type=jnp.float32)
    grad_partial = summed_over(grad_local, "node", last=4)
    back_rows = jnp.einsum(
        "io,boj->bij", weight_half, slope_all, preferred_element_type=jnp.float32
    ).astype(jnp.bfloat16)
    back_sources = jnp.einsum(
        "tb,bfj->tfj", pick_row, back_rows, preferred_element_type=jnp.float32
    ).astype(jnp.bfloat16)
    back_terms = jnp.einsum(
        "tfj,tjk->tfk", back_sources, tile_values, preferred_element_type=jnp.float32
    )
    outgoing = summed_by_table(add_source, back_terms, "ts,tfk->sfk")
    outgoing = outgoing.reshape(2 * REACH + 1, blocks, width_local, tile_size)
    feature_grad = outgoing[REACH]
    received = []
    for distance in range(-REACH, REACH + 1):
        if distance != 0:
            sent = outgoing[distance + REACH].astype(jnp.bfloat16)
            received.append(passed_along(sent, "node", distance))
    grad_partial, activated, received[0] = lax.optimization_barrier(
        (grad_partial, activated, received[0])
    )
    grad = summed_over(grad_partial, "node", first=4) * (1.0 / math.sqrt(node_total))
    for piece in received:
        feature_grad = feature_grad + piece.astype(jnp.float32)
    new_first = first_decay * first_moment + (1.0 - first_decay) * grad
    new_second = second_decay * second_moment + (1.0 - second_decay) * grad * grad
    new_weight = weight - learn_rate * (new_first / first_fix) / (
        jnp.sqrt(new_second / second_fix) + adam_eps
    )
    return (activated, feature_grad, new_weight, new_first, new_second)


def solution(mesh):
    return jax.shard_map(
        per_device,
        mesh=mesh,
        in_specs=(
            P("node", "feat", None),
            P("node", None, None),
            P("node"),
            P("node"),
            P("node"),
            P("feat", None),
            P("feat", None),
            P("feat", None),
            P("node", "feat", None),
        ),
        out_specs=(
            P("node", "feat", None),
            P("node", "feat", None),
            P("feat", None),
            P("feat", None),
            P("feat", None),
        ),
        check_vma=False,
    )
```
